256 devices in a mesh: dp: 32 (over y, x, core), mp: 8 (over z).
Axes of the slice: x: 4, y: 4, z: 8, core: 2. Of those that a mesh axis runs over, the one named last changes fastest.
Arguments:
- weights: float32 [8, 2657088], P('mp', 'dp'), may hold values from -60 to 60
- moment_first: float32 [8, 2657088], P('mp', 'dp'), may hold values from -0.6 to 0.6
- moment_second: float32 [8, 2657088], P('mp', 'dp'), may hold values from 0.01 to 1
- gradients: bfloat16 [8, 2657088], P('mp', 'dp'), may hold values from -6 to 6
- tensor_order: int32 [7], replicated, may hold values from 0 to 6, each once
Outputs:
- new_weights: float32 [8, 2657088], P('mp', 'dp')
- new_first: float32 [8, 2657088], P('mp', 'dp')
- new_second: float32 [8, 2657088], P('mp', 'dp')
- scaled_update: float32 [8, 2657088], P('mp', 'dp')
- training_copy: bfloat16 [8, 2657088], P('mp')
- trust: float32 [7], replicated
The draws below stay inside these ranges and needn't reach their ends.
Inputs may be any that keep to these rules, and one draw needn't show every extreme that they name: `tensor_order`: a permutation of 0 to 6.
All inputs are finite; a program needn't handle non-finite values.
Results may differ from the reference program's by a relative error of at most 0.0075.
Values may be sent and summed in bfloat16 or wider, within the bound.
No kernel may reach another device: no remote copies, remote signals or barrier semaphores. Data moves between devices by JAX's collectives and lax.ppermute only.
A program may use at most 192 MiB of HBM per device.

```python
import math
import jax
import jax.numpy as jnp
from jax import lax

D = 2304
EXPERTS = 8
SLOTS = 7
ROW = 2657088
N_MP = 8


def draw_weights(key, part):
    spot = lax.broadcasted_iota(jnp.int32, (N_MP, ROW), 1).astype(jnp.float32)
    frac = spot / float(ROW)
    base = jnp.clip(jax.random.normal(key, (N_MP, ROW), jnp.float32), -6.0, 6.0)
    scale = jnp.exp(math.log(10.0) * frac)
    return base * scale


def block_scale(rng, extent, cuts, smallest, high):
    def one(dim, blocks):
        heights = jax.random.uniform(jax.random.fold_in(jax.random.fold_in(rng, 6), dim), (blocks,), jnp.float32, smallest / len(cuts), high / len(cuts))
        return jnp.repeat(jnp.exp(heights), extent[dim] // blocks).reshape((-1,) + (1,) * (len(extent) - dim - 1))

    loudness = one(*cuts[0])
    for cut in cuts[1:]:
        loudness = loudness * one(*cut)
    return loudness


def gaussian(own_key, extent, deviation, limit, pieces=(), kind=jnp.bfloat16):
    values = jax.random.normal(own_key, extent, jnp.float32) * deviation
    if len(pieces) > 0:
        values = block_scale(own_key, extent, pieces, -0.22, 0.18) * values
    return jnp.clip(values, min=-limit, max=limit).astype(kind)


def setup_inputs(seed: int = 0) -> dict:
    keys = jax.random.split(jax.random.key(seed), 6)
    return {
        "weights": draw_weights(jax.random.fold_in(keys[5], 71), 0),
        "moment_first": gaussian(keys[1], (N_MP, ROW), 0.1, 0.6, ((0, 8), (1, 32)), jnp.float32),
        "moment_second": jnp.clip(jnp.exp(math.log(1.0) - 4.6051702 * jax.random.uniform(keys[2], (N_MP, ROW), jnp.float32) ** block_scale(keys[2], (N_MP, ROW), ((0, 8), (1, 32)), -0.2, 0.2)), 0.01, 1.0),
        "gradients": gaussian(keys[3], (N_MP, ROW), 1.0, 6.0, ((0, 8), (1, 32))),
        "tensor_order": jax.random.permutation(keys[4], SLOTS).astype(jnp.int32),
    }


fix_first = 1.0 - math.exp(1000.0 * math.log(0.9))
fix_second = 1.0 - math.exp(1000.0 * math.log(0.999))
decay_values = (0.01, 0.01, 0.01, 0.01, 0.0, 0.0, 0.0)
step_rate = 0.1

def tensor_kind(places, order, parts):
    lengths = jnp.array([D * D // parts] * 4 + [EXPERTS * D // parts, D // parts, D // parts], jnp.int32)
    kinds = jnp.arange(SLOTS, dtype=jnp.int32)
    slot_lengths = lax.optimization_barrier(jnp.sum(jnp.where(order[:, None] == kinds[None, :], lengths[None, :], 0), axis=1)).astype(jnp.int32)
    boundary = jnp.cumsum(slot_lengths).astype(jnp.int32)
    slot = jnp.zeros_like(places)
    for number in range(SLOTS - 1):
        slot = slot + (places >= boundary[number]).astype(jnp.int32)
    result = jnp.zeros_like(places)
    for number in range(SLOTS):
        result = jnp.where(slot == number, order[number], result)
    return result

def per_entry(kind, table):
    result = jnp.zeros(kind.shape, jnp.float32)
    for number in range(SLOTS):
        result = jnp.where(kind == number, table[number], result)
    return result

def reference(weights, moment_first, moment_second, gradients, tensor_order):
    places = jnp.broadcast_to(jnp.arange(ROW, dtype=jnp.int32)[None, :], (N_MP, ROW))
    kind = tensor_kind(places, tensor_order, N_MP)
    grads = gradients.astype(jnp.float32)
    new_first = 0.9 * moment_first + 0.1 * grads
    new_second = 0.999 * moment_second + 0.001 * grads * grads
    decay = per_entry(kind, jnp.array(decay_values, jnp.float32))
    raw = new_first / fix_first / (jnp.sqrt(new_second / fix_second) + 1e-06) + decay * weights
    flat_kind = kind.ravel()
    wsq = jax.ops.segment_sum((weights * weights).ravel(), flat_kind, num_segments=SLOTS)
    usq = jax.ops.segment_sum((raw * raw).ravel(), flat_kind, num_segments=SLOTS)
    trust = jnp.sqrt(wsq) / (jnp.sqrt(usq) + 1e-06)
    scaled_update = per_entry(kind, trust) * raw
    new_weights = weights - step_rate * scaled_update
    training_copy = new_weights.astype(jnp.bfloat16)
    return (new_weights, new_first, new_second, scaled_update, training_copy, trust)
```

```python
import math

import jax
import jax.numpy as jnp
from jax import lax
from jax.sharding import PartitionSpec as P

D = 2304
EXPERTS = 8
SLOTS = 7


fix_first = 1.0 - math.exp(1000.0 * math.log(0.9))
fix_second = 1.0 - math.exp(1000.0 * math.log(0.999))
decay_values = (0.01, 0.01, 0.01, 0.01, 0.0, 0.0, 0.0)
step_rate = 0.1


def tensor_kind(places, order, parts):
    lengths = jnp.array(
        [D * D // parts] * 4 + [EXPERTS * D // parts, D // parts, D // parts], jnp.int32
    )
    kinds = jnp.arange(SLOTS, dtype=jnp.int32)
    slot_lengths = jnp.sum(jnp.where(order[:, None] == kinds[None, :], lengths[None, :], 0), axis=1)
    boundary = jnp.cumsum(slot_lengths)
    slot = jnp.zeros_like(places)
    for number in range(SLOTS - 1):
        slot = slot + (places >= boundary[number]).astype(jnp.int32)
    result = jnp.zeros_like(places)
    for number in range(SLOTS):
        result = jnp.where(slot == number, order[number], result)
    return result


def per_entry(kind, table):
    result = jnp.zeros(kind.shape, jnp.float32)
    for number in range(SLOTS):
        result = jnp.where(kind == number, table[number], result)
    return result


def kind_sums(kind, values):
    kinds = jnp.arange(SLOTS, dtype=jnp.int32)[:, None]
    return jnp.sum(jnp.where(kind == kinds, values, 0.0), axis=1)


def tree_sum(x, axis):
    size = lax.axis_size(axis)
    step = 1
    while step < size:
        pairs = [(i, i ^ step) for i in range(size)]
        x = x + lax.ppermute(x, axis, pairs)
        step *= 2
    return x


def gather_row(piece, axis):
    width = piece.shape[1]
    padded = -(-width // 2048) * 2048
    dense = jnp.pad(piece[0], (0, padded - width)).reshape(padded // 128, 128)
    whole = lax.all_gather(dense, axis, axis=0, tiled=False)
    return whole.reshape(whole.shape[0], padded)[:, :width].reshape(1, -1)


def on_device(weights, moment_first, moment_second, gradients, tensor_order):
    parts = lax.axis_size("mp")
    width = weights.shape[1]
    places = lax.axis_index("dp") * width + lax.broadcasted_iota(jnp.int32, (1, width), 1)
    kind = tensor_kind(places, tensor_order, parts)
    wpart = kind_sums(kind, weights * weights)
    grads = gradients.astype(jnp.float32)
    new_first = 0.9 * moment_first + 0.1 * grads
    new_second = 0.999 * moment_second + 0.001 * grads * grads
    decay = per_entry(kind, jnp.array(decay_values, jnp.float32))
    raw = new_first / fix_first / (jnp.sqrt(new_second / fix_second) + 1e-06) + decay * weights
    upart = kind_sums(kind, raw * raw)
    both = tree_sum(tree_sum(jnp.concatenate([wpart, upart]), "dp"), "mp")
    wsq, usq = both[:SLOTS], both[SLOTS:]
    trust = jnp.sqrt(wsq) / (jnp.sqrt(usq) + 1e-06)
    scaled_update = per_entry(kind, trust) * raw
    new_weights = weights - step_rate * scaled_update
    training_copy = gather_row(new_weights.astype(jnp.bfloat16), "dp")
    return (new_weights, new_first, new_second, scaled_update, training_copy, trust)


def solution(mesh):
    return jax.shard_map(
        on_device,
        mesh=mesh,
        in_specs=(P("mp", "dp"), P("mp", "dp"), P("mp", "dp"), P("mp", "dp"), P()),
        out_specs=(P("mp", "dp"), P("mp", "dp"), P("mp", "dp"), P("mp", "dp"), P("mp", None), P()),
        check_vma=False,
    )
```

```python
import math

import jax
import jax.numpy as jnp
from jax import lax
from jax.sharding import PartitionSpec as P

D = 2304
EXPERTS = 8
SLOTS = 7


fix_first = 1.0 - math.exp(1000.0 * math.log(0.9))
fix_second = 1.0 - math.exp(1000.0 * math.log(0.999))
decay_values = (0.01, 0.01, 0.01, 0.01, 0.0, 0.0, 0.0)
step_rate = 0.1


def tensor_kind(places, order, parts):
    lengths = jnp.array(
        [D * D // parts] * 4 + [EXPERTS * D // parts, D // parts, D // parts], jnp.int32
    )
    kinds = jnp.arange(SLOTS, dtype=jnp.int32)
    slot_lengths = jnp.sum(jnp.where(order[:, None] == kinds[None, :], lengths[None, :], 0), axis=1)
    boundary = jnp.cumsum(slot_lengths)
    slot = jnp.zeros_like(places)
    for number in range(SLOTS - 1):
        slot = slot + (places >= boundary[number]).astype(jnp.int32)
    result = jnp.zeros_like(places)
    for number in range(SLOTS):
        result = jnp.where(slot == number, order[number], result)
    return result


def per_entry(kind, table):
    result = jnp.zeros(kind.shape, jnp.float32)
    for number in range(SLOTS):
        result = jnp.where(kind == number, table[number], result)
    return result


def kind_sums(kind, values):
    return jnp.stack([jnp.sum(jnp.where(kind == k, values, 0.0)) for k in range(SLOTS)])


def tree_sum(x, axis):
    size = lax.axis_size(axis)
    step = 1
    while step < size:
        pairs = [(i, i ^ step) for i in range(size)]
        x = x + lax.ppermute(x, axis, pairs)
        step *= 2
    return x


def to_dense(row, padded):
    return jnp.pad(row[0], (0, padded - row.shape[1])).reshape(padded // 128, 128)


def from_dense(block, width):
    return block.reshape(-1)[:width].reshape(1, width)


def on_device(weights, moment_first, moment_second, gradients, tensor_order):
    parts = lax.axis_size("mp")
    width = weights.shape[1]
    padded = -(-width // 2048) * 2048
    w = to_dense(weights, padded)
    m1 = to_dense(moment_first, padded)
    m2 = to_dense(moment_second, padded)
    grads = to_dense(gradients, padded).astype(jnp.float32)
    rows = padded // 128
    places = (
        lax.axis_index("dp") * width
        + lax.broadcasted_iota(jnp.int32, (rows, 128), 0) * 128
        + lax.broadcasted_iota(jnp.int32, (rows, 128), 1)
    )
    kind = tensor_kind(places, tensor_order, parts)
    new_first = 0.9 * m1 + 0.1 * grads
    new_second = 0.999 * m2 + 0.001 * grads * grads
    decay = per_entry(kind, jnp.array(decay_values, jnp.float32))
    raw = new_first / fix_first / (jnp.sqrt(new_second / fix_second) + 1e-06) + decay * w
    wpart = kind_sums(kind, w * w)
    upart = kind_sums(kind, raw * raw)
    both = tree_sum(tree_sum(jnp.concatenate([wpart, upart]), "dp"), "mp")
    wsq, usq = both[:SLOTS], both[SLOTS:]
    trust = jnp.sqrt(wsq) / (jnp.sqrt(usq) + 1e-06)
    scaled_update = per_entry(kind, trust) * raw
    new_weights = w - step_rate * scaled_update
    whole = lax.all_gather(new_weights.astype(jnp.bfloat16), "dp", axis=0, tiled=False)
    training_copy = whole.reshape(whole.shape[0], padded)[:, :width].reshape(1, -1)
    return (
        from_dense(new_weights, width),
        from_dense(new_first, width),
        from_dense(new_second, width),
        from_dense(scaled_update, width),
        training_copy,
        trust,
    )


def solution(mesh):
    return jax.shard_map(
        on_device,
        mesh=mesh,
        in_specs=(P("mp", "dp"), P("mp", "dp"), P("mp", "dp"), P("mp", "dp"), P()),
        out_specs=(P("mp", "dp"), P("mp", "dp"), P("mp", "dp"), P("mp", "dp"), P("mp", None), P()),
        check_vma=False,
    )
```

```python
import math

import jax
import jax.numpy as jnp
from jax import lax
from jax.sharding import PartitionSpec as P

D = 2304
EXPERTS = 8
SLOTS = 7


fix_first = 1.0 - math.exp(1000.0 * math.log(0.9))
fix_second = 1.0 - math.exp(1000.0 * math.log(0.999))
decay_values = (0.01, 0.01, 0.01, 0.01, 0.0, 0.0, 0.0)
step_rate = 0.1


def tensor_kind(places, order, parts):
    lengths = jnp.array(
        [D * D // parts] * 4 + [EXPERTS * D // parts, D // parts, D // parts], jnp.int32
    )
    kinds = jnp.arange(SLOTS, dtype=jnp.int32)
    slot_lengths = jnp.sum(jnp.where(order[:, None] == kinds[None, :], lengths[None, :], 0), axis=1)
    boundary = jnp.cumsum(slot_lengths)
    slot = jnp.zeros_like(places)
    for number in range(SLOTS - 1):
        slot = slot + (places >= boundary[number]).astype(jnp.int32)
    result = jnp.zeros_like(places)
    for number in range(SLOTS):
        result = jnp.where(slot == number, order[number], result)
    return result


def per_entry(kind, table):
    result = jnp.zeros(kind.shape, jnp.float32)
    for number in range(SLOTS):
        result = jnp.where(kind == number, table[number], result)
    return result


def kind_sums(kind, values):
    kinds = jnp.arange(SLOTS, dtype=jnp.int32)[:, None, None]
    return jnp.sum(jnp.where(kind[None] == kinds, values[None], 0.0), axis=1)


def tree_sum(x, axis):
    size = lax.axis_size(axis)
    step = 1
    while step < size:
        pairs = [(i, i ^ step) for i in range(size)]
        x = x + lax.ppermute(x, axis, pairs)
        step *= 2
    return x


def to_dense(row, padded):
    return jnp.pad(row[0], (0, padded - row.shape[1])).reshape(padded // 128, 128)


def from_dense(block, width):
    return block.reshape(-1)[:width].reshape(1, width)


def on_device(weights, moment_first, moment_second, gradients, tensor_order):
    parts = lax.axis_size("mp")
    width = weights.shape[1]
    padded = -(-width // 2048) * 2048
    w = to_dense(weights, padded)
    m1 = to_dense(moment_first, padded)
    m2 = to_dense(moment_second, padded)
    grads = to_dense(gradients, padded).astype(jnp.float32)
    rows = padded // 128
    places = (
        lax.axis_index("dp") * width
        + lax.broadcasted_iota(jnp.int32, (rows, 128), 0) * 128
        + lax.broadcasted_iota(jnp.int32, (rows, 128), 1)
    )
    kind = tensor_kind(places, tensor_order, parts)
    new_first = 0.9 * m1 + 0.1 * grads
    new_second = 0.999 * m2 + 0.001 * grads * grads
    decay = per_entry(kind, jnp.array(decay_values, jnp.float32))
    raw = new_first / fix_first / (jnp.sqrt(new_second / fix_second) + 1e-06) + decay * w
    wpart = kind_sums(kind, w * w)
    upart = kind_sums(kind, raw * raw)
    both = tree_sum(tree_sum(jnp.concatenate([wpart, upart]), "dp"), "mp")
    both = jnp.sum(both, axis=1)
    wsq, usq = both[:SLOTS], both[SLOTS:]
    trust = jnp.sqrt(wsq) / (jnp.sqrt(usq) + 1e-06)
    scaled_update = per_entry(kind, trust) * raw
    new_weights = w - step_rate * scaled_update
    whole = lax.all_gather(new_weights.astype(jnp.bfloat16), "dp", axis=0, tiled=False)
    training_copy = whole.reshape(whole.shape[0], padded)[:, :width].reshape(1, -1)
    return (
        from_dense(new_weights, width),
        from_dense(new_first, width),
        from_dense(new_second, width),
        from_dense(scaled_update, width),
        training_copy,
        trust,
    )


def solution(mesh):
    return jax.shard_map(
        on_device,
        mesh=mesh,
        in_specs=(P("mp", "dp"), P("mp", "dp"), P("mp", "dp"), P("mp", "dp"), P()),
        out_specs=(P("mp", "dp"), P("mp", "dp"), P("mp", "dp"), P("mp", "dp"), P("mp", None), P()),
        check_vma=False,
    )
```

```python
import math

import jax
import jax.numpy as jnp
from jax import lax
from jax.experimental import pallas as pl
from jax.experimental.pallas import tpu as pltpu
from jax.sharding import PartitionSpec as P

D = 2304
EXPERTS = 8
SLOTS = 7


fix_first = 1.0 - math.exp(1000.0 * math.log(0.9))
fix_second = 1.0 - math.exp(1000.0 * math.log(0.999))
decay_values = (0.01, 0.01, 0.01, 0.01, 0.0, 0.0, 0.0)
step_rate = 0.1


def tensor_kind(places, order, parts):
    lengths = jnp.array(
        [D * D // parts] * 4 + [EXPERTS * D // parts, D // parts, D // parts], jnp.int32
    )
    kinds = jnp.arange(SLOTS, dtype=jnp.int32)
    slot_lengths = jnp.sum(jnp.where(order[:, None] == kinds[None, :], lengths[None, :], 0), axis=1)
    boundary = jnp.cumsum(slot_lengths)
    slot = jnp.zeros_like(places)
    for number in range(SLOTS - 1):
        slot = slot + (places >= boundary[number]).astype(jnp.int32)
    result = jnp.zeros_like(places)
    for number in range(SLOTS):
        result = jnp.where(slot == number, order[number], result)
    return result


def per_entry(kind, table):
    result = jnp.zeros(kind.shape, jnp.float32)
    for number in range(SLOTS):
        result = jnp.where(kind == number, table[number], result)
    return result


def kind_sums(kind, values):
    kinds = jnp.arange(SLOTS, dtype=jnp.int32)[:, None, None]
    return jnp.sum(jnp.where(kind[None] == kinds, values[None], 0.0), axis=1)


def tree_sum(x, axis):
    size = lax.axis_size(axis)
    step = 1
    while step < size:
        pairs = [(i, i ^ step) for i in range(size)]
        x = x + lax.ppermute(x, axis, pairs)
        step *= 2
    return x


def to_dense(row, padded):
    return jnp.pad(row[0], (0, padded - row.shape[1])).reshape(padded // 128, 128)


def from_dense(block, width):
    return block.reshape(-1)[:width].reshape(1, width)


def slot_of(scalars_ref, rows):
    places = (
        scalars_ref[SLOTS - 1]
        + lax.broadcasted_iota(jnp.int32, (rows, 128), 0) * 128
        + lax.broadcasted_iota(jnp.int32, (rows, 128), 1)
    )
    slot = jnp.zeros((rows, 128), jnp.int32)
    for number in range(SLOTS - 1):
        slot = slot + (places >= scalars_ref[number]).astype(jnp.int32)
    return slot


def per_slot(slot, table_ref):
    result = jnp.zeros(slot.shape, jnp.float32)
    for number in range(SLOTS):
        result = jnp.where(slot == number, table_ref[number], result)
    return result


def moments_kernel(scalars_ref, decay_ref, w_ref, m1_ref, m2_ref, g_ref, nf_ref, ns_ref, raw_ref, sums_ref):
    rows = w_ref.shape[0]
    slot = slot_of(scalars_ref, rows)
    grads = g_ref[...].astype(jnp.float32)
    new_first = 0.9 * m1_ref[...] + 0.1 * grads
    new_second = 0.999 * m2_ref[...] + 0.001 * grads * grads
    w = w_ref[...]
    raw = new_first / fix_first / (jnp.sqrt(new_second / fix_second) + 1e-06) + per_slot(slot, decay_ref) * w
    nf_ref[...] = new_first
    ns_ref[...] = new_second
    raw_ref[...] = raw
    wsq = w * w
    usq = raw * raw
    sums_ref[...] = jnp.zeros(sums_ref.shape, jnp.float32)
    for number in range(SLOTS):
        mask = slot == number
        sums_ref[pl.ds(number, 1), :] = jnp.sum(jnp.where(mask, wsq, 0.0), axis=0, keepdims=True)
        sums_ref[pl.ds(8 + number, 1), :] = jnp.sum(jnp.where(mask, usq, 0.0), axis=0, keepdims=True)


def update_kernel(scalars_ref, trust_ref, w_ref, raw_ref, su_ref, nw_ref, tc_ref):
    rows = w_ref.shape[0]
    slot = slot_of(scalars_ref, rows)
    scaled_update = per_slot(slot, trust_ref) * raw_ref[...]
    new_weights = w_ref[...] - step_rate * scaled_update
    su_ref[...] = scaled_update
    nw_ref[...] = new_weights
    tc_ref[...] = new_weights.astype(jnp.bfloat16)


SMEM = pl.BlockSpec(memory_space=pltpu.SMEM)
VMEM = pl.BlockSpec(memory_space=pltpu.VMEM)


def on_device(weights, moment_first, moment_second, gradients, tensor_order):
    parts = lax.axis_size("mp")
    width = weights.shape[1]
    padded = -(-width // 2048) * 2048
    rows = padded // 128
    w = to_dense(weights, padded)
    m1 = to_dense(moment_first, padded)
    m2 = to_dense(moment_second, padded)
    g = to_dense(gradients, padded)
    lengths = jnp.array(
        [D * D // parts] * 4 + [EXPERTS * D // parts, D // parts, D // parts], jnp.int32
    )
    kinds = jnp.arange(SLOTS, dtype=jnp.int32)
    matches = tensor_order[:, None] == kinds[None, :]
    slot_lengths = jnp.sum(jnp.where(matches, lengths[None, :], 0), axis=1)
    boundary = jnp.cumsum(slot_lengths)
    scalars = jnp.concatenate(
        [boundary[: SLOTS - 1], (lax.axis_index("dp") * width)[None], jnp.zeros((1,), jnp.int32)]
    ).astype(jnp.int32)
    decay_slot = jnp.sum(jnp.where(matches, jnp.array(decay_values, jnp.float32)[None, :], 0.0), axis=1)
    dense = jax.ShapeDtypeStruct((rows, 128), jnp.float32)
    new_first, new_second, raw, sums = pl.pallas_call(
        moments_kernel,
        out_shape=(dense, dense, dense, jax.ShapeDtypeStruct((16, 128), jnp.float32)),
        in_specs=[SMEM, SMEM, VMEM, VMEM, VMEM, VMEM],
        out_specs=(VMEM, VMEM, VMEM, VMEM),
    )(scalars, decay_slot, w, m1, m2, g)
    total = jnp.sum(tree_sum(tree_sum(sums, "dp"), "mp"), axis=1)
    wsq_slot, usq_slot = total[:SLOTS], total[8 : 8 + SLOTS]
    wsq = jnp.sum(jnp.where(matches, wsq_slot[:, None], 0.0), axis=0)
    usq = jnp.sum(jnp.where(matches, usq_slot[:, None], 0.0), axis=0)
    trust = jnp.sqrt(wsq) / (jnp.sqrt(usq) + 1e-06)
    trust_slot = jnp.sum(jnp.where(matches, trust[None, :], 0.0), axis=1)
    scaled_update, new_weights, piece = pl.pallas_call(
        update_kernel,
        out_shape=(dense, dense, jax.ShapeDtypeStruct((rows, 128), jnp.bfloat16)),
        in_specs=[SMEM, SMEM, VMEM, VMEM],
        out_specs=(VMEM, VMEM, VMEM),
    )(scalars, trust_slot, w, raw)
    whole = lax.all_gather(piece, "dp", axis=0, tiled=False)
    training_copy = whole.reshape(whole.shape[0], padded)[:, :width].reshape(1, -1)
    return (
        from_dense(new_weights, width),
        from_dense(new_first, width),
        from_dense(new_second, width),
        from_dense(scaled_update, width),
        training_copy,
        trust,
    )


def solution(mesh):
    return jax.shard_map(
        on_device,
        mesh=mesh,
        in_specs=(P("mp", "dp"), P("mp", "dp"), P("mp", "dp"), P("mp", "dp"), P()),
        out_specs=(P("mp", "dp"), P("mp", "dp"), P("mp", "dp"), P("mp", "dp"), P("mp", None), P()),
        check_vma=False,
    )
```

```python
import math

import jax
import jax.numpy as jnp
from jax import lax
from jax.experimental import pallas as pl
from jax.experimental.pallas import tpu as pltpu
from jax.sharding import PartitionSpec as P

D = 2304
EXPERTS = 8
SLOTS = 7


fix_first = 1.0 - math.exp(1000.0 * math.log(0.9))
fix_second = 1.0 - math.exp(1000.0 * math.log(0.999))
decay_values = (0.01, 0.01, 0.01, 0.01, 0.0, 0.0, 0.0)
step_rate = 0.1


def tensor_kind(places, order, parts):
    lengths = jnp.array(
        [D * D // parts] * 4 + [EXPERTS * D // parts, D // parts, D // parts], jnp.int32
    )
    kinds = jnp.arange(SLOTS, dtype=jnp.int32)
    slot_lengths = jnp.sum(jnp.where(order[:, None] == kinds[None, :], lengths[None, :], 0), axis=1)
    boundary = jnp.cumsum(slot_lengths)
    slot = jnp.zeros_like(places)
    for number in range(SLOTS - 1):
        slot = slot + (places >= boundary[number]).astype(jnp.int32)
    result = jnp.zeros_like(places)
    for number in range(SLOTS):
        result = jnp.where(slot == number, order[number], result)
    return result


def per_entry(kind, table):
    result = jnp.zeros(kind.shape, jnp.float32)
    for number in range(SLOTS):
        result = jnp.where(kind == number, table[number], result)
    return result


def kind_sums(kind, values):
    kinds = jnp.arange(SLOTS, dtype=jnp.int32)[:, None, None]
    return jnp.sum(jnp.where(kind[None] == kinds, values[None], 0.0), axis=1)


def tree_sum(x, axis):
    size = lax.axis_size(axis)
    step = 1
    while step < size:
        pairs = [(i, i ^ step) for i in range(size)]
        x = x + lax.ppermute(x, axis, pairs)
        step *= 2
    return x


def to_dense(row, padded):
    return jnp.pad(row, ((0, 0), (0, padded - row.shape[1]))).reshape(padded // 128, 128)


def from_dense(block, width):
    return block.reshape(1, -1)[:, :width]


def slot_of(scalars_ref, rows):
    places = (
        scalars_ref[SLOTS - 1]
        + lax.broadcasted_iota(jnp.int32, (rows, 128), 0) * 128
        + lax.broadcasted_iota(jnp.int32, (rows, 128), 1)
    )
    slot = jnp.zeros((rows, 128), jnp.int32)
    for number in range(SLOTS - 1):
        slot = slot + (places >= scalars_ref[number]).astype(jnp.int32)
    return slot


def per_slot(slot, table_ref):
    result = jnp.zeros(slot.shape, jnp.float32)
    for number in range(SLOTS):
        result = jnp.where(slot == number, table_ref[number], result)
    return result


def moments_kernel(scalars_ref, decay_ref, w_ref, m1_ref, m2_ref, g_ref, nf_ref, ns_ref, raw_ref, sums_ref):
    rows = w_ref.shape[0]
    slot = slot_of(scalars_ref, rows)
    grads = g_ref[...].astype(jnp.float32)
    new_first = 0.9 * m1_ref[...] + 0.1 * grads
    new_second = 0.999 * m2_ref[...] + 0.001 * grads * grads
    w = w_ref[...]
    raw = new_first / fix_first / (jnp.sqrt(new_second / fix_second) + 1e-06) + per_slot(slot, decay_ref) * w
    nf_ref[...] = new_first
    ns_ref[...] = new_second
    raw_ref[...] = raw
    wsq = w * w
    usq = raw * raw
    sums_ref[...] = jnp.zeros(sums_ref.shape, jnp.float32)
    for number in range(SLOTS):
        mask = slot == number
        sums_ref[pl.ds(number, 1), :] = jnp.sum(jnp.where(mask, wsq, 0.0), axis=0, keepdims=True)
        sums_ref[pl.ds(8 + number, 1), :] = jnp.sum(jnp.where(mask, usq, 0.0), axis=0, keepdims=True)


def update_kernel(scalars_ref, trust_ref, w_ref, raw_ref, su_ref, nw_ref, tc_ref):
    rows = w_ref.shape[0]
    slot = slot_of(scalars_ref, rows)
    scaled_update = per_slot(slot, trust_ref) * raw_ref[...]
    new_weights = w_ref[...] - step_rate * scaled_update
    su_ref[...] = scaled_update
    nw_ref[...] = new_weights
    tc_ref[...] = new_weights.astype(jnp.bfloat16)


SMEM = pl.BlockSpec(memory_space=pltpu.SMEM)
VMEM = pl.BlockSpec(memory_space=pltpu.VMEM)


def on_device(weights, moment_first, moment_second, gradients, tensor_order):
    parts = lax.axis_size("mp")
    width = weights.shape[1]
    padded = -(-width // 2048) * 2048
    rows = padded // 128
    w = to_dense(weights, padded)
    m1 = to_dense(moment_first, padded)
    m2 = to_dense(moment_second, padded)
    g = to_dense(gradients, padded)
    lengths = jnp.array(
        [D * D // parts] * 4 + [EXPERTS * D // parts, D // parts, D // parts], jnp.int32
    )
    kinds = jnp.arange(SLOTS, dtype=jnp.int32)
    matches = tensor_order[:, None] == kinds[None, :]
    slot_lengths = jnp.sum(jnp.where(matches, lengths[None, :], 0), axis=1)
    boundary = jnp.cumsum(slot_lengths)
    scalars = jnp.concatenate(
        [boundary[: SLOTS - 1], (lax.axis_index("dp") * width)[None], jnp.zeros((1,), jnp.int32)]
    ).astype(jnp.int32)
    decay_slot = jnp.sum(jnp.where(matches, jnp.array(decay_values, jnp.float32)[None, :], 0.0), axis=1)
    dense = jax.ShapeDtypeStruct((rows, 128), jnp.float32)
    new_first, new_second, raw, sums = pl.pallas_call(
        moments_kernel,
        out_shape=(dense, dense, dense, jax.ShapeDtypeStruct((16, 128), jnp.float32)),
        in_specs=[SMEM, SMEM, VMEM, VMEM, VMEM, VMEM],
        out_specs=(VMEM, VMEM, VMEM, VMEM),
    )(scalars, decay_slot, w, m1, m2, g)
    total = jnp.sum(tree_sum(tree_sum(sums, "dp"), "mp"), axis=1)
    wsq_slot, usq_slot = total[:SLOTS], total[8 : 8 + SLOTS]
    wsq = jnp.sum(jnp.where(matches, wsq_slot[:, None], 0.0), axis=0)
    usq = jnp.sum(jnp.where(matches, usq_slot[:, None], 0.0), axis=0)
    trust = jnp.sqrt(wsq) / (jnp.sqrt(usq) + 1e-06)
    trust_slot = jnp.sum(jnp.where(matches, trust[None, :], 0.0), axis=1)
    scaled_update, new_weights, piece = pl.pallas_call(
        update_kernel,
        out_shape=(dense, dense, jax.ShapeDtypeStruct((rows, 128), jnp.bfloat16)),
        in_specs=[SMEM, SMEM, VMEM, VMEM],
        out_specs=(VMEM, VMEM, VMEM),
    )(scalars, trust_slot, w, raw)
    whole = lax.all_gather(piece, "dp", axis=0, tiled=False)
    training_copy = whole.reshape(whole.shape[0], padded)[:, :width].reshape(1, -1)
    return (
        from_dense(new_weights, width),
        from_dense(new_first, width),
        from_dense(new_second, width),
        from_dense(scaled_update, width),
        training_copy,
        trust,
    )


def solution(mesh):
    return jax.shard_map(
        on_device,
        mesh=mesh,
        in_specs=(P("mp", "dp"), P("mp", "dp"), P("mp", "dp"), P("mp", "dp"), P()),
        out_specs=(P("mp", "dp"), P("mp", "dp"), P("mp", "dp"), P("mp", "dp"), P("mp", None), P()),
        check_vma=False,
    )
```

```python
import functools
import math

import jax
import jax.numpy as jnp
from jax import lax
from jax.experimental import pallas as pl
from jax.experimental.pallas import tpu as pltpu
from jax.sharding import PartitionSpec as P

D = 2304
EXPERTS = 8
SLOTS = 7


fix_first = 1.0 - math.exp(1000.0 * math.log(0.9))
fix_second = 1.0 - math.exp(1000.0 * math.log(0.999))
decay_values = (0.01, 0.01, 0.01, 0.01, 0.0, 0.0, 0.0)
step_rate = 0.1


def tensor_kind(places, order, parts):
    lengths = jnp.array(
        [D * D // parts] * 4 + [EXPERTS * D // parts, D // parts, D // parts], jnp.int32
    )
    kinds = jnp.arange(SLOTS, dtype=jnp.int32)
    slot_lengths = jnp.sum(jnp.where(order[:, None] == kinds[None, :], lengths[None, :], 0), axis=1)
    boundary = jnp.cumsum(slot_lengths)
    slot = jnp.zeros_like(places)
    for number in range(SLOTS - 1):
        slot = slot + (places >= boundary[number]).astype(jnp.int32)
    result = jnp.zeros_like(places)
    for number in range(SLOTS):
        result = jnp.where(slot == number, order[number], result)
    return result


def per_entry(kind, table):
    result = jnp.zeros(kind.shape, jnp.float32)
    for number in range(SLOTS):
        result = jnp.where(kind == number, table[number], result)
    return result


def kind_sums(kind, values):
    kinds = jnp.arange(SLOTS, dtype=jnp.int32)[:, None, None]
    return jnp.sum(jnp.where(kind[None] == kinds, values[None], 0.0), axis=1)


def tree_sum(x, axis):
    size = lax.axis_size(axis)
    step = 1
    while step < size:
        pairs = [(i, i ^ step) for i in range(size)]
        x = x + lax.ppermute(x, axis, pairs)
        step *= 2
    return x


def to_dense(row, padded):
    return jnp.pad(row, ((0, 0), (0, padded - row.shape[1]))).reshape(padded // 128, 128)


def from_dense(block, width):
    return block.reshape(1, -1)[:, :width]


def slot_of(scalars_ref, rows):
    places = (
        scalars_ref[SLOTS - 1]
        + lax.broadcasted_iota(jnp.int32, (rows, 128), 0) * 128
        + lax.broadcasted_iota(jnp.int32, (rows, 128), 1)
    )
    slot = jnp.zeros((rows, 128), jnp.int32)
    for number in range(SLOTS - 1):
        slot = slot + (places >= scalars_ref[number]).astype(jnp.int32)
    return slot


def per_slot(slot, table_ref):
    result = jnp.zeros(slot.shape, jnp.float32)
    for number in range(SLOTS):
        result = jnp.where(slot == number, table_ref[number], result)
    return result


def moments_kernel(scalars_ref, decay_ref, w_ref, m1_ref, m2_ref, g_ref, nf_ref, ns_ref, raw_ref, sums_ref):
    rows = w_ref.shape[0]
    slot = slot_of(scalars_ref, rows)
    grads = g_ref[...].astype(jnp.float32)
    new_first = 0.9 * m1_ref[...] + 0.1 * grads
    new_second = 0.999 * m2_ref[...] + 0.001 * grads * grads
    w = w_ref[...]
    raw = new_first / fix_first / (jnp.sqrt(new_second / fix_second) + 1e-06) + per_slot(slot, decay_ref) * w
    nf_ref[...] = new_first
    ns_ref[...] = new_second
    raw_ref[...] = raw
    wsq = w * w
    usq = raw * raw
    sums_ref[...] = jnp.zeros(sums_ref.shape, jnp.float32)
    for number in range(SLOTS):
        mask = slot == number
        sums_ref[pl.ds(number, 1), :] = jnp.sum(jnp.where(mask, wsq, 0.0), axis=0, keepdims=True)
        sums_ref[pl.ds(8 + number, 1), :] = jnp.sum(jnp.where(mask, usq, 0.0), axis=0, keepdims=True)


def update_kernel(scalars_ref, trust_ref, w_ref, raw_ref, su_ref, nw_ref, tc_ref):
    rows = w_ref.shape[0]
    slot = slot_of(scalars_ref, rows)
    scaled_update = per_slot(slot, trust_ref) * raw_ref[...]
    new_weights = w_ref[...] - step_rate * scaled_update
    su_ref[...] = scaled_update
    nw_ref[...] = new_weights
    tc_ref[...] = new_weights.astype(jnp.bfloat16)


def assemble_kernel(width, whole_ref, out_ref):
    count, rows, _ = whole_ref.shape
    total = count * width
    lane = lax.broadcasted_iota(jnp.int32, (rows, 128), 1)
    for k in range(count):
        start, shift = divmod(k * width, 128)
        chunks = -(-(shift + width) // 128)
        piece = whole_ref[k].astype(jnp.float32)
        if shift:
            rolled = pltpu.roll(piece, shift, 1)
            piece = jnp.where(lane >= shift, rolled, pltpu.roll(rolled, 1, 0))
        if shift and k:
            held = out_ref[:, pl.ds(start * 128, 128)].astype(jnp.float32)
            first = jnp.where(lane[:1] >= shift, piece[:1], held)
            piece = jnp.concatenate([first, piece[1:]], axis=0)
        full = min(chunks, total // 128 - start)
        out_ref[:, pl.ds(start * 128, full * 128)] = piece[:full].reshape(1, full * 128).astype(out_ref.dtype)
        tail = total - (start + full) * 128
        if full < chunks and tail:
            out_ref[:, pl.ds((start + full) * 128, tail)] = piece[full : full + 1, :tail].astype(out_ref.dtype)


def assemble(whole, width):
    count = whole.shape[0]
    return pl.pallas_call(
        functools.partial(assemble_kernel, width),
        out_shape=jax.ShapeDtypeStruct((1, count * width), jnp.bfloat16),
        in_specs=[pl.BlockSpec(memory_space=pltpu.VMEM)],
        out_specs=pl.BlockSpec(memory_space=pltpu.VMEM),
    )(whole)


SMEM = pl.BlockSpec(memory_space=pltpu.SMEM)
VMEM = pl.BlockSpec(memory_space=pltpu.VMEM)


def on_device(weights, moment_first, moment_second, gradients, tensor_order):
    parts = lax.axis_size("mp")
    width = weights.shape[1]
    padded = -(-width // 2048) * 2048
    rows = padded // 128
    w = to_dense(weights, padded)
    m1 = to_dense(moment_first, padded)
    m2 = to_dense(moment_second, padded)
    g = to_dense(gradients, padded)
    lengths = jnp.array(
        [D * D // parts] * 4 + [EXPERTS * D // parts, D // parts, D // parts], jnp.int32
    )
    kinds = jnp.arange(SLOTS, dtype=jnp.int32)
    matches = tensor_order[:, None] == kinds[None, :]
    slot_lengths = jnp.sum(jnp.where(matches, lengths[None, :], 0), axis=1)
    boundary = jnp.cumsum(slot_lengths)
    scalars = jnp.concatenate(
        [boundary[: SLOTS - 1], (lax.axis_index("dp") * width)[None], jnp.zeros((1,), jnp.int32)]
    ).astype(jnp.int32)
    decay_slot = jnp.sum(jnp.where(matches, jnp.array(decay_values, jnp.float32)[None, :], 0.0), axis=1)
    dense = jax.ShapeDtypeStruct((rows, 128), jnp.float32)
    new_first, new_second, raw, sums = pl.pallas_call(
        moments_kernel,
        out_shape=(dense, dense, dense, jax.ShapeDtypeStruct((16, 128), jnp.float32)),
        in_specs=[SMEM, SMEM, VMEM, VMEM, VMEM, VMEM],
        out_specs=(VMEM, VMEM, VMEM, VMEM),
    )(scalars, decay_slot, w, m1, m2, g)
    total = jnp.sum(tree_sum(tree_sum(sums, "dp"), "mp"), axis=1)
    wsq_slot, usq_slot = total[:SLOTS], total[8 : 8 + SLOTS]
    wsq = jnp.sum(jnp.where(matches, wsq_slot[:, None], 0.0), axis=0)
    usq = jnp.sum(jnp.where(matches, usq_slot[:, None], 0.0), axis=0)
    trust = jnp.sqrt(wsq) / (jnp.sqrt(usq) + 1e-06)
    trust_slot = jnp.sum(jnp.where(matches, trust[None, :], 0.0), axis=1)
    scaled_update, new_weights, piece = pl.pallas_call(
        update_kernel,
        out_shape=(dense, dense, jax.ShapeDtypeStruct((rows, 128), jnp.bfloat16)),
        in_specs=[SMEM, SMEM, VMEM, VMEM],
        out_specs=(VMEM, VMEM, VMEM),
    )(scalars, trust_slot, w, raw)
    whole = lax.all_gather(piece, "dp", axis=0, tiled=False)
    training_copy = assemble(whole, width)
    return (
        from_dense(new_weights, width),
        from_dense(new_first, width),
        from_dense(new_second, width),
        from_dense(scaled_update, width),
        training_copy,
        trust,
    )


def solution(mesh):
    return jax.shard_map(
        on_device,
        mesh=mesh,
        in_specs=(P("mp", "dp"), P("mp", "dp"), P("mp", "dp"), P("mp", "dp"), P()),
        out_specs=(P("mp", "dp"), P("mp", "dp"), P("mp", "dp"), P("mp", "dp"), P("mp", None), P()),
        check_vma=False,
    )
```

```python
import functools
import math

import jax
import jax.numpy as jnp
from jax import lax
from jax.experimental import pallas as pl
from jax.experimental.pallas import tpu as pltpu
from jax.sharding import PartitionSpec as P

D = 2304
EXPERTS = 8
SLOTS = 7


fix_first = 1.0 - math.exp(1000.0 * math.log(0.9))
fix_second = 1.0 - math.exp(1000.0 * math.log(0.999))
decay_values = (0.01, 0.01, 0.01, 0.01, 0.0, 0.0, 0.0)
step_rate = 0.1


def tensor_kind(places, order, parts):
    lengths = jnp.array(
        [D * D // parts] * 4 + [EXPERTS * D // parts, D // parts, D // parts], jnp.int32
    )
    kinds = jnp.arange(SLOTS, dtype=jnp.int32)
    slot_lengths = jnp.sum(jnp.where(order[:, None] == kinds[None, :], lengths[None, :], 0), axis=1)
    boundary = jnp.cumsum(slot_lengths)
    slot = jnp.zeros_like(places)
    for number in range(SLOTS - 1):
        slot = slot + (places >= boundary[number]).astype(jnp.int32)
    result = jnp.zeros_like(places)
    for number in range(SLOTS):
        result = jnp.where(slot == number, order[number], result)
    return result


def per_entry(kind, table):
    result = jnp.zeros(kind.shape, jnp.float32)
    for number in range(SLOTS):
        result = jnp.where(kind == number, table[number], result)
    return result


def kind_sums(kind, values):
    kinds = jnp.arange(SLOTS, dtype=jnp.int32)[:, None, None]
    return jnp.sum(jnp.where(kind[None] == kinds, values[None], 0.0), axis=1)


def tree_sum(x, axis):
    size = lax.axis_size(axis)
    step = 1
    while step < size:
        pairs = [(i, i ^ step) for i in range(size)]
        x = x + lax.ppermute(x, axis, pairs)
        step *= 2
    return x


def to_dense(row, padded):
    return jnp.pad(row, ((0, 0), (0, padded - row.shape[1]))).reshape(padded // 128, 128)


def from_dense(block, width):
    return block.reshape(1, -1)[:, :width]


def slot_of(scalars_ref, rows):
    places = (
        scalars_ref[SLOTS - 1]
        + lax.broadcasted_iota(jnp.int32, (rows, 128), 0) * 128
        + lax.broadcasted_iota(jnp.int32, (rows, 128), 1)
    )
    slot = jnp.zeros((rows, 128), jnp.int32)
    for number in range(SLOTS - 1):
        slot = slot + (places >= scalars_ref[number]).astype(jnp.int32)
    return slot


def per_slot(slot, table_ref):
    result = jnp.zeros(slot.shape, jnp.float32)
    for number in range(SLOTS):
        result = jnp.where(slot == number, table_ref[number], result)
    return result


def load_dense(row_ref, rows, width):
    block = row_ref[...].astype(jnp.float32).reshape(rows, 128)
    inside = (
        lax.broadcasted_iota(jnp.int32, (rows, 128), 0) * 128
        + lax.broadcasted_iota(jnp.int32, (rows, 128), 1)
    ) < width
    return jnp.where(inside, block, 0.0)


def store_row(row_ref, block):
    row_ref[...] = block.reshape(row_ref.shape).astype(row_ref.dtype)


def moments_kernel(width, scalars_ref, decay_ref, w_ref, m1_ref, m2_ref, g_ref, nf_ref, ns_ref, raw_ref, sums_ref):
    rows = raw_ref.shape[0]
    slot = slot_of(scalars_ref, rows)
    grads = load_dense(g_ref, rows, width)
    new_first = 0.9 * load_dense(m1_ref, rows, width) + 0.1 * grads
    new_second = 0.999 * load_dense(m2_ref, rows, width) + 0.001 * grads * grads
    w = load_dense(w_ref, rows, width)
    raw = new_first / fix_first / (jnp.sqrt(new_second / fix_second) + 1e-06) + per_slot(slot, decay_ref) * w
    store_row(nf_ref, new_first)
    store_row(ns_ref, new_second)
    raw_ref[...] = raw
    wsq = w * w
    usq = raw * raw
    sums_ref[...] = jnp.zeros(sums_ref.shape, jnp.float32)
    for number in range(SLOTS):
        mask = slot == number
        sums_ref[pl.ds(number, 1), :] = jnp.sum(jnp.where(mask, wsq, 0.0), axis=0, keepdims=True)
        sums_ref[pl.ds(8 + number, 1), :] = jnp.sum(jnp.where(mask, usq, 0.0), axis=0, keepdims=True)


def update_kernel(width, scalars_ref, trust_ref, w_ref, raw_ref, su_ref, nw_ref, tc_ref):
    rows = raw_ref.shape[0]
    slot = slot_of(scalars_ref, rows)
    scaled_update = per_slot(slot, trust_ref) * raw_ref[...]
    new_weights = load_dense(w_ref, rows, width) - step_rate * scaled_update
    store_row(su_ref, scaled_update)
    store_row(nw_ref, new_weights)
    tc_ref[...] = new_weights.astype(jnp.bfloat16)


def assemble_kernel(width, whole_ref, out_ref):
    count, rows, _ = whole_ref.shape
    total = count * width
    lane = lax.broadcasted_iota(jnp.int32, (rows, 128), 1)
    for k in range(count):
        start, shift = divmod(k * width, 128)
        chunks = -(-(shift + width) // 128)
        piece = whole_ref[k].astype(jnp.float32)
        if shift:
            rolled = pltpu.roll(piece, shift, 1)
            piece = jnp.where(lane >= shift, rolled, pltpu.roll(rolled, 1, 0))
        if shift and k:
            held = out_ref[:, pl.ds(start * 128, 128)].astype(jnp.float32)
            first = jnp.where(lane[:1] >= shift, piece[:1], held)
            piece = jnp.concatenate([first, piece[1:]], axis=0)
        full = min(chunks, total // 128 - start)
        out_ref[:, pl.ds(start * 128, full * 128)] = piece[:full].reshape(1, full * 128).astype(out_ref.dtype)
        tail = total - (start + full) * 128
        if full < chunks and tail:
            out_ref[:, pl.ds((start + full) * 128, tail)] = piece[full : full + 1, :tail].astype(out_ref.dtype)


def assemble(whole, width):
    count = whole.shape[0]
    return pl.pallas_call(
        functools.partial(assemble_kernel, width),
        out_shape=jax.ShapeDtypeStruct((1, count * width), jnp.bfloat16),
        in_specs=[pl.BlockSpec(memory_space=pltpu.VMEM)],
        out_specs=pl.BlockSpec(memory_space=pltpu.VMEM),
    )(whole)


def on_device(weights, moment_first, moment_second, gradients, tensor_order):
    parts = lax.axis_size("mp")
    width = weights.shape[1]
    padded = -(-width // 2048) * 2048
    rows = padded // 128
    lengths = jnp.array(
        [D * D // parts] * 4 + [EXPERTS * D // parts, D // parts, D // parts], jnp.int32
    )
    kinds = jnp.arange(SLOTS, dtype=jnp.int32)
    matches = tensor_order[:, None] == kinds[None, :]
    slot_lengths = jnp.sum(jnp.where(matches, lengths[None, :], 0), axis=1)
    boundary = jnp.cumsum(slot_lengths)
    scalars = jnp.concatenate(
        [boundary[: SLOTS - 1], (lax.axis_index("dp") * width)[None], jnp.zeros((1,), jnp.int32)]
    ).astype(jnp.int32)
    decay_slot = jnp.sum(jnp.where(matches, jnp.array(decay_values, jnp.float32)[None, :], 0.0), axis=1)
    dense = jax.ShapeDtypeStruct((rows, 128), jnp.float32)
    row = jax.ShapeDtypeStruct((1, width), jnp.float32)
    row_block = pl.BlockSpec((1, padded), lambda i: (0, 0))
    whole_block = lambda shape: pl.BlockSpec(shape, lambda i: (0, 0))
    scalar_block = pl.BlockSpec(memory_space=pltpu.SMEM)
    new_first, new_second, raw, sums = pl.pallas_call(
        functools.partial(moments_kernel, width),
        grid=(1,),
        out_shape=(row, row, dense, jax.ShapeDtypeStruct((16, 128), jnp.float32)),
        in_specs=[scalar_block, scalar_block, row_block, row_block, row_block, row_block],
        out_specs=(row_block, row_block, whole_block((rows, 128)), whole_block((16, 128))),
    )(scalars, decay_slot, weights, moment_first, moment_second, gradients)
    total = jnp.sum(tree_sum(tree_sum(sums, "dp"), "mp"), axis=1)
    wsq_slot, usq_slot = total[:SLOTS], total[8 : 8 + SLOTS]
    wsq = jnp.sum(jnp.where(matches, wsq_slot[:, None], 0.0), axis=0)
    usq = jnp.sum(jnp.where(matches, usq_slot[:, None], 0.0), axis=0)
    trust = jnp.sqrt(wsq) / (jnp.sqrt(usq) + 1e-06)
    trust_slot = jnp.sum(jnp.where(matches, trust[None, :], 0.0), axis=1)
    scaled_update, new_weights, piece = pl.pallas_call(
        functools.partial(update_kernel, width),
        grid=(1,),
        out_shape=(row, row, jax.ShapeDtypeStruct((rows, 128), jnp.bfloat16)),
        in_specs=[scalar_block, scalar_block, row_block, whole_block((rows, 128))],
        out_specs=(row_block, row_block, whole_block((rows, 128))),
    )(scalars, trust_slot, weights, raw)
    whole = lax.all_gather(piece, "dp", axis=0, tiled=False)
    training_copy = assemble(whole, width)
    return (new_weights, new_first, new_second, scaled_update, training_copy, trust)


def solution(mesh):
    return jax.shard_map(
        on_device,
        mesh=mesh,
        in_specs=(P("mp", "dp"), P("mp", "dp"), P("mp", "dp"), P("mp", "dp"), P()),
        out_specs=(P("mp", "dp"), P("mp", "dp"), P("mp", "dp"), P("mp", "dp"), P("mp", None), P()),
        check_vma=False,
    )
```

```python
import functools
import math

import jax
import jax.numpy as jnp
from jax import lax
from jax.experimental import pallas as pl
from jax.experimental.pallas import tpu as pltpu
from jax.sharding import PartitionSpec as P

D = 2304
EXPERTS = 8
SLOTS = 7


fix_first = 1.0 - math.exp(1000.0 * math.log(0.9))
fix_second = 1.0 - math.exp(1000.0 * math.log(0.999))
decay_values = (0.01, 0.01, 0.01, 0.01, 0.0, 0.0, 0.0)
step_rate = 0.1


def tensor_kind(places, order, parts):
    lengths = jnp.array(
        [D * D // parts] * 4 + [EXPERTS * D // parts, D // parts, D // parts], jnp.int32
    )
    kinds = jnp.arange(SLOTS, dtype=jnp.int32)
    slot_lengths = jnp.sum(jnp.where(order[:, None] == kinds[None, :], lengths[None, :], 0), axis=1)
    boundary = jnp.cumsum(slot_lengths)
    slot = jnp.zeros_like(places)
    for number in range(SLOTS - 1):
        slot = slot + (places >= boundary[number]).astype(jnp.int32)
    result = jnp.zeros_like(places)
    for number in range(SLOTS):
        result = jnp.where(slot == number, order[number], result)
    return result


def per_entry(kind, table):
    result = jnp.zeros(kind.shape, jnp.float32)
    for number in range(SLOTS):
        result = jnp.where(kind == number, table[number], result)
    return result


def kind_sums(kind, values):
    kinds = jnp.arange(SLOTS, dtype=jnp.int32)[:, None, None]
    return jnp.sum(jnp.where(kind[None] == kinds, values[None], 0.0), axis=1)


def tree_sum(x, axis):
    size = lax.axis_size(axis)
    step = 1
    while step < size:
        pairs = [(i, i ^ step) for i in range(size)]
        x = x + lax.ppermute(x, axis, pairs)
        step *= 2
    return x


def to_dense(row, padded):
    return jnp.pad(row, ((0, 0), (0, padded - row.shape[1]))).reshape(padded // 128, 128)


def from_dense(block, width):
    return block.reshape(1, -1)[:, :width]


def slot_of(order_ref, width, parts, rows):
    lengths = [D * D // parts] * 4 + [EXPERTS * D // parts, D // parts, D // parts]
    places = (
        lax.axis_index("dp") * width
        + lax.broadcasted_iota(jnp.int32, (rows, 128), 0) * 128
        + lax.broadcasted_iota(jnp.int32, (rows, 128), 1)
    )
    slot = jnp.zeros((rows, 128), jnp.int32)
    boundary = jnp.int32(0)
    for number in range(SLOTS - 1):
        kind = order_ref[number]
        length = jnp.int32(lengths[SLOTS - 1])
        for other in range(SLOTS - 1):
            length = jnp.where(kind == other, jnp.int32(lengths[other]), length)
        boundary = boundary + length
        slot = slot + (places >= boundary).astype(jnp.int32)
    return slot


def decay_of(order_ref, slot):
    result = jnp.zeros(slot.shape, jnp.float32)
    for number in range(SLOTS):
        kind = order_ref[number]
        value = jnp.float32(0.0)
        for other in range(SLOTS):
            value = jnp.where(kind == other, jnp.float32(decay_values[other]), value)
        result = jnp.where(slot == number, value, result)
    return result


def load_dense(row_ref, rows, width):
    block = row_ref[...].astype(jnp.float32).reshape(rows, 128)
    inside = (
        lax.broadcasted_iota(jnp.int32, (rows, 128), 0) * 128
        + lax.broadcasted_iota(jnp.int32, (rows, 128), 1)
    ) < width
    return jnp.where(inside, block, 0.0)


def store_row(row_ref, block):
    row_ref[...] = block.reshape(row_ref.shape).astype(row_ref.dtype)


def moments_kernel(width, parts, order_ref, w_ref, m1_ref, m2_ref, g_ref, nf_ref, ns_ref, raw_ref, sums_ref):
    rows = raw_ref.shape[0]
    slot = slot_of(order_ref, width, parts, rows)
    grads = load_dense(g_ref, rows, width)
    new_first = 0.9 * load_dense(m1_ref, rows, width) + 0.1 * grads
    new_second = 0.999 * load_dense(m2_ref, rows, width) + 0.001 * grads * grads
    w = load_dense(w_ref, rows, width)
    raw = new_first / fix_first / (jnp.sqrt(new_second / fix_second) + 1e-06) + decay_of(order_ref, slot) * w
    store_row(nf_ref, new_first)
    store_row(ns_ref, new_second)
    raw_ref[...] = raw
    wsq = w * w
    usq = raw * raw
    sums_ref[...] = jnp.zeros(sums_ref.shape, jnp.float32)
    for number in range(SLOTS):
        mask = slot == number
        sums_ref[pl.ds(number, 1), :] = jnp.sum(jnp.where(mask, wsq, 0.0), axis=0, keepdims=True)
        sums_ref[pl.ds(8 + number, 1), :] = jnp.sum(jnp.where(mask, usq, 0.0), axis=0, keepdims=True)


def update_kernel(width, parts, order_ref, total_ref, w_ref, raw_ref, su_ref, nw_ref, tc_ref):
    rows = raw_ref.shape[0]
    slot = slot_of(order_ref, width, parts, rows)
    sums = jnp.sum(total_ref[...], axis=1, keepdims=True)
    trust = jnp.sqrt(sums[:8]) / (jnp.sqrt(sums[8:]) + 1e-06)
    factor = jnp.zeros((rows, 128), jnp.float32)
    for number in range(SLOTS):
        factor = jnp.where(slot == number, trust[number : number + 1, :], factor)
    scaled_update = factor * raw_ref[...]
    new_weights = load_dense(w_ref, rows, width) - step_rate * scaled_update
    store_row(su_ref, scaled_update)
    store_row(nw_ref, new_weights)
    tc_ref[...] = new_weights.astype(jnp.bfloat16)


def assemble_kernel(width, whole_ref, out_ref):
    count, rows, _ = whole_ref.shape
    total = count * width
    lane = lax.broadcasted_iota(jnp.int32, (rows, 128), 1)
    for k in range(count):
        start, shift = divmod(k * width, 128)
        chunks = -(-(shift + width) // 128)
        piece = whole_ref[k].astype(jnp.float32)
        if shift:
            rolled = pltpu.roll(piece, shift, 1)
            piece = jnp.where(lane >= shift, rolled, pltpu.roll(rolled, 1, 0))
        if shift and k:
            held = out_ref[:, pl.ds(start * 128, 128)].astype(jnp.float32)
            first = jnp.where(lane[:1] >= shift, piece[:1], held)
            piece = jnp.concatenate([first, piece[1:]], axis=0)
        full = min(chunks, total // 128 - start)
        out_ref[:, pl.ds(start * 128, full * 128)] = piece[:full].reshape(1, full * 128).astype(out_ref.dtype)
        tail = total - (start + full) * 128
        if full < chunks and tail:
            out_ref[:, pl.ds((start + full) * 128, tail)] = piece[full : full + 1, :tail].astype(out_ref.dtype)


def assemble(whole, width):
    count = whole.shape[0]
    return pl.pallas_call(
        functools.partial(assemble_kernel, width),
        out_shape=jax.ShapeDtypeStruct((1, count * width), jnp.bfloat16),
        in_specs=[pl.BlockSpec(memory_space=pltpu.VMEM)],
        out_specs=pl.BlockSpec(memory_space=pltpu.VMEM),
    )(whole)


def on_device(weights, moment_first, moment_second, gradients, tensor_order):
    parts = lax.axis_size("mp")
    width = weights.shape[1]
    padded = -(-width // 2048) * 2048
    rows = padded // 128
    dense = jax.ShapeDtypeStruct((rows, 128), jnp.float32)
    row = jax.ShapeDtypeStruct((1, width), jnp.float32)
    row_block = pl.BlockSpec((1, padded), lambda i: (0, 0))
    whole_block = lambda shape: pl.BlockSpec(shape, lambda i: (0, 0))
    scalar_block = pl.BlockSpec(memory_space=pltpu.SMEM)
    new_first, new_second, raw, sums = pl.pallas_call(
        functools.partial(moments_kernel, width, parts),
        grid=(1,),
        out_shape=(row, row, dense, jax.ShapeDtypeStruct((16, 128), jnp.float32)),
        in_specs=[scalar_block, row_block, row_block, row_block, row_block],
        out_specs=(row_block, row_block, whole_block((rows, 128)), whole_block((16, 128))),
    )(tensor_order, weights, moment_first, moment_second, gradients)
    total = tree_sum(tree_sum(sums, "dp"), "mp")
    scaled_update, new_weights, piece = pl.pallas_call(
        functools.partial(update_kernel, width, parts),
        grid=(1,),
        out_shape=(row, row, jax.ShapeDtypeStruct((rows, 128), jnp.bfloat16)),
        in_specs=[scalar_block, whole_block((16, 128)), row_block, whole_block((rows, 128))],
        out_specs=(row_block, row_block, whole_block((rows, 128))),
    )(tensor_order, total, weights, raw)
    whole = lax.all_gather(piece, "dp", axis=0, tiled=False)
    training_copy = assemble(whole, width)
    sums_by_slot = jnp.sum(total, axis=1)
    matches = tensor_order[:, None] == jnp.arange(SLOTS, dtype=jnp.int32)[None, :]
    wsq = jnp.sum(jnp.where(matches, sums_by_slot[:SLOTS, None], 0.0), axis=0)
    usq = jnp.sum(jnp.where(matches, sums_by_slot[8 : 8 + SLOTS, None], 0.0), axis=0)
    trust = jnp.sqrt(wsq) / (jnp.sqrt(usq) + 1e-06)
    return (new_weights, new_first, new_second, scaled_update, training_copy, trust)


def solution(mesh):
    return jax.shard_map(
        on_device,
        mesh=mesh,
        in_specs=(P("mp", "dp"), P("mp", "dp"), P("mp", "dp"), P("mp", "dp"), P()),
        out_specs=(P("mp", "dp"), P("mp", "dp"), P("mp", "dp"), P("mp", "dp"), P("mp", None), P()),
        check_vma=False,
    )
```

```python
import functools
import math

import jax
import jax.numpy as jnp
from jax import lax
from jax.experimental import pallas as pl
from jax.experimental.pallas import tpu as pltpu
from jax.sharding import PartitionSpec as P

D = 2304
EXPERTS = 8
SLOTS = 7


fix_first = 1.0 - math.exp(1000.0 * math.log(0.9))
fix_second = 1.0 - math.exp(1000.0 * math.log(0.999))
decay_values = (0.01, 0.01, 0.01, 0.01, 0.0, 0.0, 0.0)
step_rate = 0.1


def tensor_kind(places, order, parts):
    lengths = jnp.array(
        [D * D // parts] * 4 + [EXPERTS * D // parts, D // parts, D // parts], jnp.int32
    )
    kinds = jnp.arange(SLOTS, dtype=jnp.int32)
    slot_lengths = jnp.sum(jnp.where(order[:, None] == kinds[None, :], lengths[None, :], 0), axis=1)
    boundary = jnp.cumsum(slot_lengths)
    slot = jnp.zeros_like(places)
    for number in range(SLOTS - 1):
        slot = slot + (places >= boundary[number]).astype(jnp.int32)
    result = jnp.zeros_like(places)
    for number in range(SLOTS):
        result = jnp.where(slot == number, order[number], result)
    return result


def per_entry(kind, table):
    result = jnp.zeros(kind.shape, jnp.float32)
    for number in range(SLOTS):
        result = jnp.where(kind == number, table[number], result)
    return result


def kind_sums(kind, values):
    kinds = jnp.arange(SLOTS, dtype=jnp.int32)[:, None, None]
    return jnp.sum(jnp.where(kind[None] == kinds, values[None], 0.0), axis=1)


def tree_sum(x, axis):
    size = lax.axis_size(axis)
    step = 1
    while step < size:
        pairs = [(i, i ^ step) for i in range(size)]
        x = x + lax.ppermute(x, axis, pairs)
        step *= 2
    return x


def to_dense(row, padded):
    return jnp.pad(row, ((0, 0), (0, padded - row.shape[1]))).reshape(padded // 128, 128)


def from_dense(block, width):
    return block.reshape(1, -1)[:, :width]


def position():
    return lax.axis_index("chips") * lax.axis_size("core") + lax.axis_index("core")


def slot_of(order_ref, width, parts, rows):
    lengths = [D * D // parts] * 4 + [EXPERTS * D // parts, D // parts, D // parts]
    places = (
        position() * width
        + lax.broadcasted_iota(jnp.int32, (rows, 128), 0) * 128
        + lax.broadcasted_iota(jnp.int32, (rows, 128), 1)
    )
    slot = jnp.zeros((rows, 128), jnp.int32)
    boundary = jnp.int32(0)
    for number in range(SLOTS - 1):
        kind = order_ref[number]
        length = jnp.int32(lengths[SLOTS - 1])
        for other in range(SLOTS - 1):
            length = jnp.where(kind == other, jnp.int32(lengths[other]), length)
        boundary = boundary + length
        slot = slot + (places >= boundary).astype(jnp.int32)
    return slot


def decay_of(order_ref, slot):
    result = jnp.zeros(slot.shape, jnp.float32)
    for number in range(SLOTS):
        kind = order_ref[number]
        value = jnp.float32(0.0)
        for other in range(SLOTS):
            value = jnp.where(kind == other, jnp.float32(decay_values[other]), value)
        result = jnp.where(slot == number, value, result)
    return result


def load_dense(row_ref, rows, width):
    block = row_ref[...].astype(jnp.float32).reshape(rows, 128)
    inside = (
        lax.broadcasted_iota(jnp.int32, (rows, 128), 0) * 128
        + lax.broadcasted_iota(jnp.int32, (rows, 128), 1)
    ) < width
    return jnp.where(inside, block, 0.0)


def store_row(row_ref, block):
    row_ref[...] = block.reshape(row_ref.shape).astype(row_ref.dtype)


def moments_kernel(width, parts, order_ref, w_ref, m1_ref, m2_ref, g_ref, nf_ref, ns_ref, raw_ref, sums_ref):
    rows = raw_ref.shape[0]
    slot = slot_of(order_ref, width, parts, rows)
    grads = load_dense(g_ref, rows, width)
    new_first = 0.9 * load_dense(m1_ref, rows, width) + 0.1 * grads
    new_second = 0.999 * load_dense(m2_ref, rows, width) + 0.001 * grads * grads
    w = load_dense(w_ref, rows, width)
    raw = new_first / fix_first / (jnp.sqrt(new_second / fix_second) + 1e-06) + decay_of(order_ref, slot) * w
    store_row(nf_ref, new_first)
    store_row(ns_ref, new_second)
    raw_ref[...] = raw
    wsq = w * w
    usq = raw * raw
    sums_ref[...] = jnp.zeros(sums_ref.shape, jnp.float32)
    for number in range(SLOTS):
        mask = slot == number
        sums_ref[pl.ds(number, 1), :] = jnp.sum(jnp.where(mask, wsq, 0.0), axis=0, keepdims=True)
        sums_ref[pl.ds(8 + number, 1), :] = jnp.sum(jnp.where(mask, usq, 0.0), axis=0, keepdims=True)


def update_kernel(width, parts, order_ref, total_ref, w_ref, raw_ref, su_ref, nw_ref, tc_ref):
    rows = raw_ref.shape[0]
    slot = slot_of(order_ref, width, parts, rows)
    sums = jnp.sum(total_ref[...], axis=1, keepdims=True)
    trust = jnp.sqrt(sums[:8]) / (jnp.sqrt(sums[8:]) + 1e-06)
    factor = jnp.zeros((rows, 128), jnp.float32)
    for number in range(SLOTS):
        factor = jnp.where(slot == number, trust[number : number + 1, :], factor)
    scaled_update = factor * raw_ref[...]
    new_weights = load_dense(w_ref, rows, width) - step_rate * scaled_update
    store_row(su_ref, scaled_update)
    store_row(nw_ref, new_weights)
    tc_ref[...] = new_weights.astype(jnp.bfloat16)


def assemble_kernel(width, mine_ref, other_ref, out_ref):
    half, rows, _ = mine_ref.shape
    count = 2 * half
    total = count * width
    core = lax.axis_index("core")
    lane = lax.broadcasted_iota(jnp.int32, (rows, 128), 1)
    for k in range(count):
        start, shift = divmod(k * width, 128)
        chunks = -(-(shift + width) // 128)
        piece = jnp.where(core == k % 2, mine_ref[k // 2], other_ref[k // 2]).astype(jnp.float32)
        if shift:
            rolled = pltpu.roll(piece, shift, 1)
            piece = jnp.where(lane >= shift, rolled, pltpu.roll(rolled, 1, 0))
        if shift and k:
            held = out_ref[:, pl.ds(start * 128, 128)].astype(jnp.float32)
            first = jnp.where(lane[:1] >= shift, piece[:1], held)
            piece = jnp.concatenate([first, piece[1:]], axis=0)
        full = min(chunks, total // 128 - start)
        out_ref[:, pl.ds(start * 128, full * 128)] = piece[:full].reshape(1, full * 128).astype(out_ref.dtype)
        tail = total - (start + full) * 128
        if full < chunks and tail:
            out_ref[:, pl.ds((start + full) * 128, tail)] = piece[full : full + 1, :tail].astype(out_ref.dtype)


def assemble(mine, other, width):
    count = 2 * mine.shape[0]
    return pl.pallas_call(
        functools.partial(assemble_kernel, width),
        out_shape=jax.ShapeDtypeStruct((1, count * width), jnp.bfloat16),
        in_specs=[pl.BlockSpec(memory_space=pltpu.VMEM)] * 2,
        out_specs=pl.BlockSpec(memory_space=pltpu.VMEM),
    )(mine, other)


def on_device(weights, moment_first, moment_second, gradients, tensor_order):
    parts = lax.axis_size("mp")
    width = weights.shape[1]
    padded = -(-width // 2048) * 2048
    rows = padded // 128
    dense = jax.ShapeDtypeStruct((rows, 128), jnp.float32)
    row = jax.ShapeDtypeStruct((1, width), jnp.float32)
    row_block = pl.BlockSpec((1, padded), lambda i: (0, 0))
    whole_block = lambda shape: pl.BlockSpec(shape, lambda i: (0, 0))
    scalar_block = pl.BlockSpec(memory_space=pltpu.SMEM)
    new_first, new_second, raw, sums = pl.pallas_call(
        functools.partial(moments_kernel, width, parts),
        grid=(1,),
        out_shape=(row, row, dense, jax.ShapeDtypeStruct((16, 128), jnp.float32)),
        in_specs=[scalar_block, row_block, row_block, row_block, row_block],
        out_specs=(row_block, row_block, whole_block((rows, 128)), whole_block((16, 128))),
    )(tensor_order, weights, moment_first, moment_second, gradients)
    total = tree_sum(tree_sum(tree_sum(sums, "core"), "chips"), "mp")
    scaled_update, new_weights, piece = pl.pallas_call(
        functools.partial(update_kernel, width, parts),
        grid=(1,),
        out_shape=(row, row, jax.ShapeDtypeStruct((rows, 128), jnp.bfloat16)),
        in_specs=[scalar_block, whole_block((16, 128)), row_block, whole_block((rows, 128))],
        out_specs=(row_block, row_block, whole_block((rows, 128))),
    )(tensor_order, total, weights, raw)
    mine = lax.all_gather(piece, "chips", axis=0, tiled=False)
    other = lax.ppermute(mine, "core", [(0, 1), (1, 0)])
    training_copy = assemble(mine, other, width)
    sums_by_slot = jnp.sum(total, axis=1)
    matches = tensor_order[:, None] == jnp.arange(SLOTS, dtype=jnp.int32)[None, :]
    wsq = jnp.sum(jnp.where(matches, sums_by_slot[:SLOTS, None], 0.0), axis=0)
    usq = jnp.sum(jnp.where(matches, sums_by_slot[8 : 8 + SLOTS, None], 0.0), axis=0)
    trust = jnp.sqrt(wsq) / (jnp.sqrt(usq) + 1e-06)
    return (new_weights, new_first, new_second, scaled_update, training_copy, trust)


def solution(mesh):
    rows, columns = mesh.devices.shape
    fine = jax.sharding.Mesh(mesh.devices.reshape(rows // 2, 2, columns), ("chips", "core", "mp"))
    shard = P("mp", ("chips", "core"))
    return jax.shard_map(
        on_device,
        mesh=fine,
        in_specs=(shard, shard, shard, shard, P()),
        out_specs=(shard, shard, shard, shard, P("mp", None), P()),
        check_vma=False,
    )
```

```python
import functools
import math

import jax
import jax.numpy as jnp
from jax import lax
from jax.experimental import pallas as pl
from jax.experimental.pallas import tpu as pltpu
from jax.sharding import PartitionSpec as P

D = 2304
EXPERTS = 8
SLOTS = 7


fix_first = 1.0 - math.exp(1000.0 * math.log(0.9))
fix_second = 1.0 - math.exp(1000.0 * math.log(0.999))
decay_values = (0.01, 0.01, 0.01, 0.01, 0.0, 0.0, 0.0)
step_rate = 0.1


def tensor_kind(places, order, parts):
    lengths = jnp.array(
        [D * D // parts] * 4 + [EXPERTS * D // parts, D // parts, D // parts], jnp.int32
    )
    kinds = jnp.arange(SLOTS, dtype=jnp.int32)
    slot_lengths = jnp.sum(jnp.where(order[:, None] == kinds[None, :], lengths[None, :], 0), axis=1)
    boundary = jnp.cumsum(slot_lengths)
    slot = jnp.zeros_like(places)
    for number in range(SLOTS - 1):
        slot = slot + (places >= boundary[number]).astype(jnp.int32)
    result = jnp.zeros_like(places)
    for number in range(SLOTS):
        result = jnp.where(slot == number, order[number], result)
    return result


def per_entry(kind, table):
    result = jnp.zeros(kind.shape, jnp.float32)
    for number in range(SLOTS):
        result = jnp.where(kind == number, table[number], result)
    return result


def kind_sums(kind, values):
    kinds = jnp.arange(SLOTS, dtype=jnp.int32)[:, None, None]
    return jnp.sum(jnp.where(kind[None] == kinds, values[None], 0.0), axis=1)


def tree_sum(x, axis):
    size = lax.axis_size(axis)
    step = 1
    while step < size:
        pairs = [(i, i ^ step) for i in range(size)]
        x = x + lax.ppermute(x, axis, pairs)
        step *= 2
    return x


def to_dense(row, padded):
    return jnp.pad(row, ((0, 0), (0, padded - row.shape[1]))).reshape(padded // 128, 128)


def from_dense(block, width):
    return block.reshape(1, -1)[:, :width]


def position():
    index = lax.axis_index("y") * lax.axis_size("x") + lax.axis_index("x")
    return index * lax.axis_size("core") + lax.axis_index("core")


def slot_of(order_ref, width, parts, rows):
    lengths = [D * D // parts] * 4 + [EXPERTS * D // parts, D // parts, D // parts]
    places = (
        position() * width
        + lax.broadcasted_iota(jnp.int32, (rows, 128), 0) * 128
        + lax.broadcasted_iota(jnp.int32, (rows, 128), 1)
    )
    slot = jnp.zeros((rows, 128), jnp.int32)
    boundary = jnp.int32(0)
    for number in range(SLOTS - 1):
        kind = order_ref[number]
        length = jnp.int32(lengths[SLOTS - 1])
        for other in range(SLOTS - 1):
            length = jnp.where(kind == other, jnp.int32(lengths[other]), length)
        boundary = boundary + length
        slot = slot + (places >= boundary).astype(jnp.int32)
    return slot


def decay_of(order_ref, slot):
    result = jnp.zeros(slot.shape, jnp.float32)
    for number in range(SLOTS):
        kind = order_ref[number]
        value = jnp.float32(0.0)
        for other in range(SLOTS):
            value = jnp.where(kind == other, jnp.float32(decay_values[other]), value)
        result = jnp.where(slot == number, value, result)
    return result


def load_dense(row_ref, rows, width):
    block = row_ref[...].astype(jnp.float32).reshape(rows, 128)
    inside = (
        lax.broadcasted_iota(jnp.int32, (rows, 128), 0) * 128
        + lax.broadcasted_iota(jnp.int32, (rows, 128), 1)
    ) < width
    return jnp.where(inside, block, 0.0)


def store_row(row_ref, block):
    row_ref[...] = block.reshape(row_ref.shape).astype(row_ref.dtype)


def moments_kernel(width, parts, order_ref, w_ref, m1_ref, m2_ref, g_ref, nf_ref, ns_ref, raw_ref, sums_ref):
    rows = raw_ref.shape[0]
    slot = slot_of(order_ref, width, parts, rows)
    grads = load_dense(g_ref, rows, width)
    new_first = 0.9 * load_dense(m1_ref, rows, width) + 0.1 * grads
    new_second = 0.999 * load_dense(m2_ref, rows, width) + 0.001 * grads * grads
    w = load_dense(w_ref, rows, width)
    raw = new_first / fix_first / (jnp.sqrt(new_second / fix_second) + 1e-06) + decay_of(order_ref, slot) * w
    store_row(nf_ref, new_first)
    store_row(ns_ref, new_second)
    raw_ref[...] = raw
    wsq = w * w
    usq = raw * raw
    sums_ref[...] = jnp.zeros(sums_ref.shape, jnp.float32)
    for number in range(SLOTS):
        mask = slot == number
        sums_ref[pl.ds(number, 1), :] = jnp.sum(jnp.where(mask, wsq, 0.0), axis=0, keepdims=True)
        sums_ref[pl.ds(8 + number, 1), :] = jnp.sum(jnp.where(mask, usq, 0.0), axis=0, keepdims=True)


def update_kernel(width, parts, order_ref, total_ref, w_ref, raw_ref, su_ref, nw_ref, tc_ref):
    rows = raw_ref.shape[0]
    slot = slot_of(order_ref, width, parts, rows)
    sums = jnp.sum(total_ref[...], axis=1, keepdims=True)
    trust = jnp.sqrt(sums[:8]) / (jnp.sqrt(sums[8:]) + 1e-06)
    factor = jnp.zeros((rows, 128), jnp.float32)
    for number in range(SLOTS):
        factor = jnp.where(slot == number, trust[number : number + 1, :], factor)
    scaled_update = factor * raw_ref[...]
    new_weights = load_dense(w_ref, rows, width) - step_rate * scaled_update
    store_row(su_ref, scaled_update)
    store_row(nw_ref, new_weights)
    tc_ref[...] = new_weights.astype(jnp.bfloat16)


def assemble_kernel(width, whole_ref, out_ref):
    count, rows, _ = whole_ref.shape
    total = count * width
    lane = lax.broadcasted_iota(jnp.int32, (rows, 128), 1)
    for k in range(count):
        start, shift = divmod(k * width, 128)
        chunks = -(-(shift + width) // 128)
        piece = whole_ref[k].astype(jnp.float32)
        if shift:
            rolled = pltpu.roll(piece, shift, 1)
            piece = jnp.where(lane >= shift, rolled, pltpu.roll(rolled, 1, 0))
        if shift and k:
            held = out_ref[:, pl.ds(start * 128, 128)].astype(jnp.float32)
            first = jnp.where(lane[:1] >= shift, piece[:1], held)
            piece = jnp.concatenate([first, piece[1:]], axis=0)
        full = min(chunks, total // 128 - start)
        out_ref[:, pl.ds(start * 128, full * 128)] = piece[:full].reshape(1, full * 128).astype(out_ref.dtype)
        tail = total - (start + full) * 128
        if full < chunks and tail:
            out_ref[:, pl.ds((start + full) * 128, tail)] = piece[full : full + 1, :tail].astype(out_ref.dtype)


def assemble(whole, width):
    count = whole.shape[0]
    return pl.pallas_call(
        functools.partial(assemble_kernel, width),
        out_shape=jax.ShapeDtypeStruct((1, count * width), jnp.bfloat16),
        in_specs=[pl.BlockSpec(memory_space=pltpu.VMEM)],
        out_specs=pl.BlockSpec(memory_space=pltpu.VMEM),
    )(whole)


def on_device(weights, moment_first, moment_second, gradients, tensor_order):
    parts = lax.axis_size("mp")
    width = weights.shape[1]
    padded = -(-width // 2048) * 2048
    rows = padded // 128
    dense = jax.ShapeDtypeStruct((rows, 128), jnp.float32)
    row = jax.ShapeDtypeStruct((1, width), jnp.float32)
    row_block = pl.BlockSpec((1, padded), lambda i: (0, 0))
    whole_block = lambda shape: pl.BlockSpec(shape, lambda i: (0, 0))
    scalar_block = pl.BlockSpec(memory_space=pltpu.SMEM)
    new_first, new_second, raw, sums = pl.pallas_call(
        functools.partial(moments_kernel, width, parts),
        grid=(1,),
        out_shape=(row, row, dense, jax.ShapeDtypeStruct((16, 128), jnp.float32)),
        in_specs=[scalar_block, row_block, row_block, row_block, row_block],
        out_specs=(row_block, row_block, whole_block((rows, 128)), whole_block((16, 128))),
    )(tensor_order, weights, moment_first, moment_second, gradients)
    total = sums
    for axis in ("core", "x", "y", "mp"):
        total = tree_sum(total, axis)
    scaled_update, new_weights, piece = pl.pallas_call(
        functools.partial(update_kernel, width, parts),
        grid=(1,),
        out_shape=(row, row, jax.ShapeDtypeStruct((rows, 128), jnp.bfloat16)),
        in_specs=[scalar_block, whole_block((16, 128)), row_block, whole_block((rows, 128))],
        out_specs=(row_block, row_block, whole_block((rows, 128))),
    )(tensor_order, total, weights, raw)
    whole = piece
    for axis in ("core", "x", "y"):
        whole = lax.all_gather(whole, axis, axis=0, tiled=False)
    whole = whole.reshape(-1, rows, 128)
    training_copy = assemble(whole, width)
    sums_by_slot = jnp.sum(total, axis=1)
    matches = tensor_order[:, None] == jnp.arange(SLOTS, dtype=jnp.int32)[None, :]
    wsq = jnp.sum(jnp.where(matches, sums_by_slot[:SLOTS, None], 0.0), axis=0)
    usq = jnp.sum(jnp.where(matches, sums_by_slot[8 : 8 + SLOTS, None], 0.0), axis=0)
    trust = jnp.sqrt(wsq) / (jnp.sqrt(usq) + 1e-06)
    return (new_weights, new_first, new_second, scaled_update, training_copy, trust)


def solution(mesh):
    ys, xs = 4, 4
    rows, columns = mesh.devices.shape
    fine = jax.sharding.Mesh(
        mesh.devices.reshape(ys, xs, rows // (ys * xs), columns), ("y", "x", "core", "mp")
    )
    shard = P("mp", ("y", "x", "core"))
    return jax.shard_map(
        on_device,
        mesh=fine,
        in_specs=(shard, shard, shard, shard, P()),
        out_specs=(shard, shard, shard, shard, P("mp", None), P()),
        check_vma=False,
    )
```

```python
import functools
import math

import jax
import jax.numpy as jnp
from jax import lax
from jax.experimental import pallas as pl
from jax.experimental.pallas import tpu as pltpu
from jax.sharding import PartitionSpec as P

D = 2304
EXPERTS = 8
SLOTS = 7


fix_first = 1.0 - math.exp(1000.0 * math.log(0.9))
fix_second = 1.0 - math.exp(1000.0 * math.log(0.999))
decay_values = (0.01, 0.01, 0.01, 0.01, 0.0, 0.0, 0.0)
step_rate = 0.1


def tensor_kind(places, order, parts):
    lengths = jnp.array(
        [D * D // parts] * 4 + [EXPERTS * D // parts, D // parts, D // parts], jnp.int32
    )
    kinds = jnp.arange(SLOTS, dtype=jnp.int32)
    slot_lengths = jnp.sum(jnp.where(order[:, None] == kinds[None, :], lengths[None, :], 0), axis=1)
    boundary = jnp.cumsum(slot_lengths)
    slot = jnp.zeros_like(places)
    for number in range(SLOTS - 1):
        slot = slot + (places >= boundary[number]).astype(jnp.int32)
    result = jnp.zeros_like(places)
    for number in range(SLOTS):
        result = jnp.where(slot == number, order[number], result)
    return result


def per_entry(kind, table):
    result = jnp.zeros(kind.shape, jnp.float32)
    for number in range(SLOTS):
        result = jnp.where(kind == number, table[number], result)
    return result


def kind_sums(kind, values):
    kinds = jnp.arange(SLOTS, dtype=jnp.int32)[:, None, None]
    return jnp.sum(jnp.where(kind[None] == kinds, values[None], 0.0), axis=1)


def tree_sum(x, axis):
    size = lax.axis_size(axis)
    step = 1
    while step < size:
        pairs = [(i, i ^ step) for i in range(size)]
        x = x + lax.ppermute(x, axis, pairs)
        step *= 2
    return x


def to_dense(row, padded):
    return jnp.pad(row, ((0, 0), (0, padded - row.shape[1]))).reshape(padded // 128, 128)


def from_dense(block, width):
    return block.reshape(1, -1)[:, :width]


def slot_of(order_ref, width, parts, rows):
    lengths = [D * D // parts] * 4 + [EXPERTS * D // parts, D // parts, D // parts]
    places = (
        lax.axis_index("dp") * width
        + lax.broadcasted_iota(jnp.int32, (rows, 128), 0) * 128
        + lax.broadcasted_iota(jnp.int32, (rows, 128), 1)
    )
    slot = jnp.zeros((rows, 128), jnp.int32)
    boundary = jnp.int32(0)
    for number in range(SLOTS - 1):
        kind = order_ref[number]
        length = jnp.int32(lengths[SLOTS - 1])
        for other in range(SLOTS - 1):
            length = jnp.where(kind == other, jnp.int32(lengths[other]), length)
        boundary = boundary + length
        slot = slot + (places >= boundary).astype(jnp.int32)
    return slot


def decay_of(order_ref, slot):
    result = jnp.zeros(slot.shape, jnp.float32)
    for number in range(SLOTS):
        kind = order_ref[number]
        value = jnp.float32(0.0)
        for other in range(SLOTS):
            value = jnp.where(kind == other, jnp.float32(decay_values[other]), value)
        result = jnp.where(slot == number, value, result)
    return result


def load_dense(row_ref, rows, width):
    block = row_ref[...].astype(jnp.float32).reshape(rows, 128)
    inside = (
        lax.broadcasted_iota(jnp.int32, (rows, 128), 0) * 128
        + lax.broadcasted_iota(jnp.int32, (rows, 128), 1)
    ) < width
    return jnp.where(inside, block, 0.0)


def store_row(row_ref, block):
    row_ref[...] = block.reshape(row_ref.shape).astype(row_ref.dtype)


def moments_kernel(width, parts, order_ref, w_ref, m1_ref, m2_ref, g_ref, nf_ref, ns_ref, raw_ref, sums_ref):
    rows = raw_ref.shape[0]
    slot = slot_of(order_ref, width, parts, rows)
    grads = load_dense(g_ref, rows, width)
    new_first = 0.9 * load_dense(m1_ref, rows, width) + 0.1 * grads
    new_second = 0.999 * load_dense(m2_ref, rows, width) + 0.001 * grads * grads
    w = load_dense(w_ref, rows, width)
    raw = new_first / fix_first / (jnp.sqrt(new_second / fix_second) + 1e-06) + decay_of(order_ref, slot) * w
    store_row(nf_ref, new_first)
    store_row(ns_ref, new_second)
    raw_ref[...] = raw
    wsq = w * w
    usq = raw * raw
    sums_ref[...] = jnp.zeros(sums_ref.shape, jnp.float32)
    for number in range(SLOTS):
        mask = slot == number
        sums_ref[pl.ds(number, 1), :] = jnp.sum(jnp.where(mask, wsq, 0.0), axis=0, keepdims=True)
        sums_ref[pl.ds(8 + number, 1), :] = jnp.sum(jnp.where(mask, usq, 0.0), axis=0, keepdims=True)


def update_kernel(width, parts, order_ref, total_ref, w_ref, raw_ref, su_ref, nw_ref, tc_ref):
    rows = raw_ref.shape[0]
    slot = slot_of(order_ref, width, parts, rows)
    sums = jnp.sum(total_ref[...], axis=1, keepdims=True)
    trust = jnp.sqrt(sums[:8]) / (jnp.sqrt(sums[8:]) + 1e-06)
    factor = jnp.zeros((rows, 128), jnp.float32)
    for number in range(SLOTS):
        factor = jnp.where(slot == number, trust[number : number + 1, :], factor)
    scaled_update = factor * raw_ref[...]
    new_weights = load_dense(w_ref, rows, width) - step_rate * scaled_update
    store_row(su_ref, scaled_update)
    store_row(nw_ref, new_weights)
    tc_ref[...] = new_weights.astype(jnp.bfloat16)


def assemble_kernel(width, whole_ref, out_ref, stage_ref, sems):
    count, rows, _ = whole_ref.shape
    total = count * width
    lane = lax.broadcasted_iota(jnp.int32, (rows, 128), 1)
    copies = []
    for k in range(count):
        start, shift = divmod(k * width, 128)
        chunks = -(-(shift + width) // 128)
        piece = whole_ref[k].astype(jnp.float32)
        if shift:
            rolled = pltpu.roll(piece, shift, 1)
            piece = jnp.where(lane >= shift, rolled, pltpu.roll(rolled, 1, 0))
        if shift and k:
            held = stage_ref[:, pl.ds(start * 128, 128)].astype(jnp.float32)
            first = jnp.where(lane[:1] >= shift, piece[:1], held)
            piece = jnp.concatenate([first, piece[1:]], axis=0)
        full = min(chunks, total // 128 - start)
        stage_ref[:, pl.ds(start * 128, full * 128)] = piece[:full].reshape(1, full * 128).astype(stage_ref.dtype)
        tail = total - (start + full) * 128
        if full < chunks and tail:
            stage_ref[:, pl.ds((start + full) * 128, tail)] = piece[full : full + 1, :tail].astype(stage_ref.dtype)
        if k + 1 < count:
            end = ((k + 1) * width) // 128 * 128
        else:
            end = total
        begin = 0 if k == 0 else copies_end
        copy = pltpu.make_async_copy(
            stage_ref.at[:, pl.ds(begin, end - begin)], out_ref.at[:, pl.ds(begin, end - begin)], sems.at[k]
        )
        copy.start()
        copies.append(copy)
        copies_end = end
    for copy in copies:
        copy.wait()


def assemble(whole, width):
    count = whole.shape[0]
    return pl.pallas_call(
        functools.partial(assemble_kernel, width),
        out_shape=jax.ShapeDtypeStruct((1, count * width), jnp.bfloat16),
        in_specs=[pl.BlockSpec(memory_space=pltpu.VMEM)],
        out_specs=pl.BlockSpec(memory_space=pl.ANY),
        scratch_shapes=[pltpu.VMEM((1, count * width), jnp.bfloat16), pltpu.SemaphoreType.DMA((count,))],
    )(whole)


def on_device(weights, moment_first, moment_second, gradients, tensor_order):
    parts = lax.axis_size("mp")
    width = weights.shape[1]
    padded = -(-width // 2048) * 2048
    rows = padded // 128
    dense = jax.ShapeDtypeStruct((rows, 128), jnp.float32)
    row = jax.ShapeDtypeStruct((1, width), jnp.float32)
    row_block = pl.BlockSpec((1, padded), lambda i: (0, 0))
    whole_block = lambda shape: pl.BlockSpec(shape, lambda i: (0, 0))
    scalar_block = pl.BlockSpec(memory_space=pltpu.SMEM)
    new_first, new_second, raw, sums = pl.pallas_call(
        functools.partial(moments_kernel, width, parts),
        grid=(1,),
        out_shape=(row, row, dense, jax.ShapeDtypeStruct((16, 128), jnp.float32)),
        in_specs=[scalar_block, row_block, row_block, row_block, row_block],
        out_specs=(row_block, row_block, whole_block((rows, 128)), whole_block((16, 128))),
    )(tensor_order, weights, moment_first, moment_second, gradients)
    total = tree_sum(tree_sum(sums, "dp"), "mp")
    scaled_update, new_weights, piece = pl.pallas_call(
        functools.partial(update_kernel, width, parts),
        grid=(1,),
        out_shape=(row, row, jax.ShapeDtypeStruct((rows, 128), jnp.bfloat16)),
        in_specs=[scalar_block, whole_block((16, 128)), row_block, whole_block((rows, 128))],
        out_specs=(row_block, row_block, whole_block((rows, 128))),
    )(tensor_order, total, weights, raw)
    whole = lax.all_gather(piece, "dp", axis=0, tiled=False)
    training_copy = assemble(whole, width)
    sums_by_slot = jnp.sum(total, axis=1)
    matches = tensor_order[:, None] == jnp.arange(SLOTS, dtype=jnp.int32)[None, :]
    wsq = jnp.sum(jnp.where(matches, sums_by_slot[:SLOTS, None], 0.0), axis=0)
    usq = jnp.sum(jnp.where(matches, sums_by_slot[8 : 8 + SLOTS, None], 0.0), axis=0)
    trust = jnp.sqrt(wsq) / (jnp.sqrt(usq) + 1e-06)
    return (new_weights, new_first, new_second, scaled_update, training_copy, trust)


def solution(mesh):
    return jax.shard_map(
        on_device,
        mesh=mesh,
        in_specs=(P("mp", "dp"), P("mp", "dp"), P("mp", "dp"), P("mp", "dp"), P()),
        out_specs=(P("mp", "dp"), P("mp", "dp"), P("mp", "dp"), P("mp", "dp"), P("mp", None), P()),
        check_vma=False,
    )
```

```python
import functools
import math

import jax
import jax.numpy as jnp
from jax import lax
from jax.experimental import pallas as pl
from jax.experimental.pallas import tpu as pltpu
from jax.sharding import PartitionSpec as P

D = 2304
EXPERTS = 8
SLOTS = 7


fix_first = 1.0 - math.exp(1000.0 * math.log(0.9))
fix_second = 1.0 - math.exp(1000.0 * math.log(0.999))
decay_values = (0.01, 0.01, 0.01, 0.01, 0.0, 0.0, 0.0)
step_rate = 0.1


def tensor_kind(places, order, parts):
    lengths = jnp.array(
        [D * D // parts] * 4 + [EXPERTS * D // parts, D // parts, D // parts], jnp.int32
    )
    kinds = jnp.arange(SLOTS, dtype=jnp.int32)
    slot_lengths = jnp.sum(jnp.where(order[:, None] == kinds[None, :], lengths[None, :], 0), axis=1)
    boundary = jnp.cumsum(slot_lengths)
    slot = jnp.zeros_like(places)
    for number in range(SLOTS - 1):
        slot = slot + (places >= boundary[number]).astype(jnp.int32)
    result = jnp.zeros_like(places)
    for number in range(SLOTS):
        result = jnp.where(slot == number, order[number], result)
    return result


def per_entry(kind, table):
    result = jnp.zeros(kind.shape, jnp.float32)
    for number in range(SLOTS):
        result = jnp.where(kind == number, table[number], result)
    return result


def kind_sums(kind, values):
    kinds = jnp.arange(SLOTS, dtype=jnp.int32)[:, None, None]
    return jnp.sum(jnp.where(kind[None] == kinds, values[None], 0.0), axis=1)


def tree_sum(x, axis):
    size = lax.axis_size(axis)
    step = 1
    while step < size:
        pairs = [(i, i ^ step) for i in range(size)]
        x = x + lax.ppermute(x, axis, pairs)
        step *= 2
    return x


def to_dense(row, padded):
    return jnp.pad(row, ((0, 0), (0, padded - row.shape[1]))).reshape(padded // 128, 128)


def from_dense(block, width):
    return block.reshape(1, -1)[:, :width]


def slot_of(order_ref, width, parts, rows):
    lengths = [D * D // parts] * 4 + [EXPERTS * D // parts, D // parts, D // parts]
    places = (
        lax.axis_index("dp") * width
        + lax.broadcasted_iota(jnp.int32, (rows, 128), 0) * 128
        + lax.broadcasted_iota(jnp.int32, (rows, 128), 1)
    )
    slot = jnp.zeros((rows, 128), jnp.int32)
    boundary = jnp.int32(0)
    for number in range(SLOTS - 1):
        kind = order_ref[number]
        length = jnp.int32(lengths[SLOTS - 1])
        for other in range(SLOTS - 1):
            length = jnp.where(kind == other, jnp.int32(lengths[other]), length)
        boundary = boundary + length
        slot = slot + (places >= boundary).astype(jnp.int32)
    return slot


def decay_of(order_ref, slot):
    result = jnp.zeros(slot.shape, jnp.float32)
    for number in range(SLOTS):
        kind = order_ref[number]
        value = jnp.float32(0.0)
        for other in range(SLOTS):
            value = jnp.where(kind == other, jnp.float32(decay_values[other]), value)
        result = jnp.where(slot == number, value, result)
    return result


def load_dense(row_ref, rows, width):
    block = row_ref[...].astype(jnp.float32).reshape(rows, 128)
    inside = (
        lax.broadcasted_iota(jnp.int32, (rows, 128), 0) * 128
        + lax.broadcasted_iota(jnp.int32, (rows, 128), 1)
    ) < width
    return jnp.where(inside, block, 0.0)


def store_row(row_ref, block):
    row_ref[...] = block.reshape(row_ref.shape).astype(row_ref.dtype)


def moments_kernel(width, parts, order_ref, w_ref, m1_ref, m2_ref, g_ref, nf_ref, ns_ref, raw_ref, sums_ref):
    rows = raw_ref.shape[0]
    slot = slot_of(order_ref, width, parts, rows)
    grads = load_dense(g_ref, rows, width)
    new_first = 0.9 * load_dense(m1_ref, rows, width) + 0.1 * grads
    new_second = 0.999 * load_dense(m2_ref, rows, width) + 0.001 * grads * grads
    w = load_dense(w_ref, rows, width)
    raw = new_first / fix_first / (jnp.sqrt(new_second / fix_second) + 1e-06) + decay_of(order_ref, slot) * w
    store_row(nf_ref, new_first)
    store_row(ns_ref, new_second)
    raw_ref[...] = raw
    wsq = w * w
    usq = raw * raw
    sums_ref[...] = jnp.zeros(sums_ref.shape, jnp.float32)
    for number in range(SLOTS):
        mask = slot == number
        sums_ref[pl.ds(number, 1), :] = jnp.sum(jnp.where(mask, wsq, 0.0), axis=0, keepdims=True)
        sums_ref[pl.ds(8 + number, 1), :] = jnp.sum(jnp.where(mask, usq, 0.0), axis=0, keepdims=True)


def update_kernel(width, parts, order_ref, total_ref, w_ref, raw_ref, su_ref, nw_ref, tc_ref):
    rows = raw_ref.shape[0]
    slot = slot_of(order_ref, width, parts, rows)
    sums = jnp.sum(total_ref[...], axis=1, keepdims=True)
    trust = jnp.sqrt(sums[:8]) / (jnp.sqrt(sums[8:]) + 1e-06)
    factor = jnp.zeros((rows, 128), jnp.float32)
    for number in range(SLOTS):
        factor = jnp.where(slot == number, trust[number : number + 1, :], factor)
    scaled_update = factor * raw_ref[...]
    new_weights = load_dense(w_ref, rows, width) - step_rate * scaled_update
    store_row(su_ref, scaled_update)
    store_row(nw_ref, new_weights)
    tc_ref[...] = new_weights.astype(jnp.bfloat16)


def assemble_kernel(width, whole_ref, out_ref, slots, stage_ref, fetch_sems, sems):
    count, rows, _ = whole_ref.shape
    total = count * width
    lane = lax.broadcasted_iota(jnp.int32, (rows, 128), 1)
    fetches = [
        pltpu.make_async_copy(whole_ref.at[k], slots.at[k % 2], fetch_sems.at[k % 2]) for k in range(count)
    ]
    fetches[0].start()
    copies = []
    for k in range(count):
        start, shift = divmod(k * width, 128)
        chunks = -(-(shift + width) // 128)
        if k + 1 < count:
            fetches[k + 1].start()
        fetches[k].wait()
        piece = slots[k % 2].astype(jnp.float32)
        if shift:
            rolled = pltpu.roll(piece, shift, 1)
            piece = jnp.where(lane >= shift, rolled, pltpu.roll(rolled, 1, 0))
        if shift and k:
            held = stage_ref[:, pl.ds(start * 128, 128)].astype(jnp.float32)
            first = jnp.where(lane[:1] >= shift, piece[:1], held)
            piece = jnp.concatenate([first, piece[1:]], axis=0)
        full = min(chunks, total // 128 - start)
        stage_ref[:, pl.ds(start * 128, full * 128)] = piece[:full].reshape(1, full * 128).astype(stage_ref.dtype)
        tail = total - (start + full) * 128
        if full < chunks and tail:
            stage_ref[:, pl.ds((start + full) * 128, tail)] = piece[full : full + 1, :tail].astype(stage_ref.dtype)
        if k + 1 < count:
            end = ((k + 1) * width) // 128 * 128
        else:
            end = total
        begin = 0 if k == 0 else copies_end
        copy = pltpu.make_async_copy(
            stage_ref.at[:, pl.ds(begin, end - begin)], out_ref.at[:, pl.ds(begin, end - begin)], sems.at[k]
        )
        copy.start()
        copies.append(copy)
        copies_end = end
    for copy in copies:
        copy.wait()


def assemble(whole, width):
    count = whole.shape[0]
    return pl.pallas_call(
        functools.partial(assemble_kernel, width),
        out_shape=jax.ShapeDtypeStruct((1, count * width), jnp.bfloat16),
        in_specs=[pl.BlockSpec(memory_space=pl.ANY)],
        out_specs=pl.BlockSpec(memory_space=pl.ANY),
        scratch_shapes=[
            pltpu.VMEM((2,) + whole.shape[1:], whole.dtype),
            pltpu.VMEM((1, count * width), jnp.bfloat16),
            pltpu.SemaphoreType.DMA((2,)),
            pltpu.SemaphoreType.DMA((count,)),
        ],
    )(whole)


def on_device(weights, moment_first, moment_second, gradients, tensor_order):
    parts = lax.axis_size("mp")
    width = weights.shape[1]
    padded = -(-width // 2048) * 2048
    rows = padded // 128
    dense = jax.ShapeDtypeStruct((rows, 128), jnp.float32)
    row = jax.ShapeDtypeStruct((1, width), jnp.float32)
    row_block = pl.BlockSpec((1, padded), lambda i: (0, 0))
    whole_block = lambda shape: pl.BlockSpec(shape, lambda i: (0, 0))
    scalar_block = pl.BlockSpec(memory_space=pltpu.SMEM)
    new_first, new_second, raw, sums = pl.pallas_call(
        functools.partial(moments_kernel, width, parts),
        grid=(1,),
        out_shape=(row, row, dense, jax.ShapeDtypeStruct((16, 128), jnp.float32)),
        in_specs=[scalar_block, row_block, row_block, row_block, row_block],
        out_specs=(row_block, row_block, whole_block((rows, 128)), whole_block((16, 128))),
    )(tensor_order, weights, moment_first, moment_second, gradients)
    total = tree_sum(tree_sum(sums, "dp"), "mp")
    scaled_update, new_weights, piece = pl.pallas_call(
        functools.partial(update_kernel, width, parts),
        grid=(1,),
        out_shape=(row, row, jax.ShapeDtypeStruct((rows, 128), jnp.bfloat16)),
        in_specs=[scalar_block, whole_block((16, 128)), row_block, whole_block((rows, 128))],
        out_specs=(row_block, row_block, whole_block((rows, 128))),
    )(tensor_order, total, weights, raw)
    whole = lax.all_gather(piece, "dp", axis=0, tiled=False)
    training_copy = assemble(whole, width)
    sums_by_slot = jnp.sum(total, axis=1)
    matches = tensor_order[:, None] == jnp.arange(SLOTS, dtype=jnp.int32)[None, :]
    wsq = jnp.sum(jnp.where(matches, sums_by_slot[:SLOTS, None], 0.0), axis=0)
    usq = jnp.sum(jnp.where(matches, sums_by_slot[8 : 8 + SLOTS, None], 0.0), axis=0)
    trust = jnp.sqrt(wsq) / (jnp.sqrt(usq) + 1e-06)
    return (new_weights, new_first, new_second, scaled_update, training_copy, trust)


def solution(mesh):
    return jax.shard_map(
        on_device,
        mesh=mesh,
        in_specs=(P("mp", "dp"), P("mp", "dp"), P("mp", "dp"), P("mp", "dp"), P()),
        out_specs=(P("mp", "dp"), P("mp", "dp"), P("mp", "dp"), P("mp", "dp"), P("mp", None), P()),
        check_vma=False,
    )
```

```python
import functools
import math

import jax
import jax.numpy as jnp
from jax import lax
from jax.experimental import pallas as pl
from jax.experimental.pallas import tpu as pltpu
from jax.sharding import PartitionSpec as P

D = 2304
EXPERTS = 8
SLOTS = 7


fix_first = 1.0 - math.exp(1000.0 * math.log(0.9))
fix_second = 1.0 - math.exp(1000.0 * math.log(0.999))
decay_values = (0.01, 0.01, 0.01, 0.01, 0.0, 0.0, 0.0)
step_rate = 0.1


def tensor_kind(places, order, parts):
    lengths = jnp.array(
        [D * D // parts] * 4 + [EXPERTS * D // parts, D // parts, D // parts], jnp.int32
    )
    kinds = jnp.arange(SLOTS, dtype=jnp.int32)
    slot_lengths = jnp.sum(jnp.where(order[:, None] == kinds[None, :], lengths[None, :], 0), axis=1)
    boundary = jnp.cumsum(slot_lengths)
    slot = jnp.zeros_like(places)
    for number in range(SLOTS - 1):
        slot = slot + (places >= boundary[number]).astype(jnp.int32)
    result = jnp.zeros_like(places)
    for number in range(SLOTS):
        result = jnp.where(slot == number, order[number], result)
    return result


def per_entry(kind, table):
    result = jnp.zeros(kind.shape, jnp.float32)
    for number in range(SLOTS):
        result = jnp.where(kind == number, table[number], result)
    return result


def kind_sums(kind, values):
    kinds = jnp.arange(SLOTS, dtype=jnp.int32)[:, None, None]
    return jnp.sum(jnp.where(kind[None] == kinds, values[None], 0.0), axis=1)


GRAY = (0, 1, 3, 2)


def partner(index, step, size):
    if size != 32:
        return index ^ step
    core, x, y = index % 2, (index // 2) % 4, index // 8
    if step == 1:
        core ^= 1
    elif step < 8:
        x = GRAY[GRAY[x] ^ (step // 2)]
    else:
        y = GRAY[GRAY[y] ^ (step // 8)]
    return (y * 4 + x) * 2 + core


def tree_sum(x, axis):
    size = lax.axis_size(axis)
    step = 1
    while step < size:
        pairs = [(i, partner(i, step, size) if axis == "dp" else i ^ step) for i in range(size)]
        x = x + lax.ppermute(x, axis, pairs)
        step *= 2
    return x


def to_dense(row, padded):
    return jnp.pad(row, ((0, 0), (0, padded - row.shape[1]))).reshape(padded // 128, 128)


def from_dense(block, width):
    return block.reshape(1, -1)[:, :width]


def slot_of(order_ref, width, parts, rows):
    lengths = [D * D // parts] * 4 + [EXPERTS * D // parts, D // parts, D // parts]
    places = (
        lax.axis_index("dp") * width
        + lax.broadcasted_iota(jnp.int32, (rows, 128), 0) * 128
        + lax.broadcasted_iota(jnp.int32, (rows, 128), 1)
    )
    slot = jnp.zeros((rows, 128), jnp.int32)
    boundary = jnp.int32(0)
    for number in range(SLOTS - 1):
        kind = order_ref[number]
        length = jnp.int32(lengths[SLOTS - 1])
        for other in range(SLOTS - 1):
            length = jnp.where(kind == other, jnp.int32(lengths[other]), length)
        boundary = boundary + length
        slot = slot + (places >= boundary).astype(jnp.int32)
    return slot


def decay_of(order_ref, slot):
    result = jnp.zeros(slot.shape, jnp.float32)
    for number in range(SLOTS):
        kind = order_ref[number]
        value = jnp.float32(0.0)
        for other in range(SLOTS):
            value = jnp.where(kind == other, jnp.float32(decay_values[other]), value)
        result = jnp.where(slot == number, value, result)
    return result


def load_dense(row_ref, rows, width):
    block = row_ref[...].astype(jnp.float32).reshape(rows, 128)
    inside = (
        lax.broadcasted_iota(jnp.int32, (rows, 128), 0) * 128
        + lax.broadcasted_iota(jnp.int32, (rows, 128), 1)
    ) < width
    return jnp.where(inside, block, 0.0)


def store_row(row_ref, block):
    row_ref[...] = block.reshape(row_ref.shape).astype(row_ref.dtype)


def moments_kernel(width, parts, order_ref, w_ref, m1_ref, m2_ref, g_ref, nf_ref, ns_ref, raw_ref, sums_ref):
    rows = raw_ref.shape[0]
    slot = slot_of(order_ref, width, parts, rows)
    grads = load_dense(g_ref, rows, width)
    new_first = 0.9 * load_dense(m1_ref, rows, width) + 0.1 * grads
    new_second = 0.999 * load_dense(m2_ref, rows, width) + 0.001 * grads * grads
    w = load_dense(w_ref, rows, width)
    raw = new_first / fix_first / (jnp.sqrt(new_second / fix_second) + 1e-06) + decay_of(order_ref, slot) * w
    store_row(nf_ref, new_first)
    store_row(ns_ref, new_second)
    raw_ref[...] = raw
    wsq = w * w
    usq = raw * raw
    sums_ref[...] = jnp.zeros(sums_ref.shape, jnp.float32)
    for number in range(SLOTS):
        mask = slot == number
        sums_ref[pl.ds(number, 1), :] = jnp.sum(jnp.where(mask, wsq, 0.0), axis=0, keepdims=True)
        sums_ref[pl.ds(8 + number, 1), :] = jnp.sum(jnp.where(mask, usq, 0.0), axis=0, keepdims=True)


def update_kernel(width, parts, order_ref, total_ref, w_ref, raw_ref, su_ref, nw_ref, tc_ref):
    rows = raw_ref.shape[0]
    slot = slot_of(order_ref, width, parts, rows)
    sums = jnp.sum(total_ref[...], axis=1, keepdims=True)
    trust = jnp.sqrt(sums[:8]) / (jnp.sqrt(sums[8:]) + 1e-06)
    factor = jnp.zeros((rows, 128), jnp.float32)
    for number in range(SLOTS):
        factor = jnp.where(slot == number, trust[number : number + 1, :], factor)
    scaled_update = factor * raw_ref[...]
    new_weights = load_dense(w_ref, rows, width) - step_rate * scaled_update
    store_row(su_ref, scaled_update)
    store_row(nw_ref, new_weights)
    tc_ref[...] = new_weights.astype(jnp.bfloat16)


def assemble_kernel(width, whole_ref, out_ref, stage_ref, sems):
    count, rows, _ = whole_ref.shape
    total = count * width
    lane = lax.broadcasted_iota(jnp.int32, (rows, 128), 1)
    copies = []
    for k in range(count):
        start, shift = divmod(k * width, 128)
        chunks = -(-(shift + width) // 128)
        piece = whole_ref[k].astype(jnp.float32)
        if shift:
            rolled = pltpu.roll(piece, shift, 1)
            piece = jnp.where(lane >= shift, rolled, pltpu.roll(rolled, 1, 0))
        if shift and k:
            held = stage_ref[:, pl.ds(start * 128, 128)].astype(jnp.float32)
            first = jnp.where(lane[:1] >= shift, piece[:1], held)
            piece = jnp.concatenate([first, piece[1:]], axis=0)
        full = min(chunks, total // 128 - start)
        stage_ref[:, pl.ds(start * 128, full * 128)] = piece[:full].reshape(1, full * 128).astype(stage_ref.dtype)
        tail = total - (start + full) * 128
        if full < chunks and tail:
            stage_ref[:, pl.ds((start + full) * 128, tail)] = piece[full : full + 1, :tail].astype(stage_ref.dtype)
        if k + 1 < count:
            end = ((k + 1) * width) // 128 * 128
        else:
            end = total
        begin = 0 if k == 0 else copies_end
        copy = pltpu.make_async_copy(
            stage_ref.at[:, pl.ds(begin, end - begin)], out_ref.at[:, pl.ds(begin, end - begin)], sems.at[k]
        )
        copy.start()
        copies.append(copy)
        copies_end = end
    for copy in copies:
        copy.wait()


def assemble(whole, width):
    count = whole.shape[0]
    return pl.pallas_call(
        functools.partial(assemble_kernel, width),
        out_shape=jax.ShapeDtypeStruct((1, count * width), jnp.bfloat16),
        in_specs=[pl.BlockSpec(memory_space=pltpu.VMEM)],
        out_specs=pl.BlockSpec(memory_space=pl.ANY),
        scratch_shapes=[pltpu.VMEM((1, count * width), jnp.bfloat16), pltpu.SemaphoreType.DMA((count,))],
    )(whole)


def on_device(weights, moment_first, moment_second, gradients, tensor_order):
    parts = lax.axis_size("mp")
    width = weights.shape[1]
    padded = -(-width // 2048) * 2048
    rows = padded // 128
    dense = jax.ShapeDtypeStruct((rows, 128), jnp.float32)
    row = jax.ShapeDtypeStruct((1, width), jnp.float32)
    row_block = pl.BlockSpec((1, padded), lambda i: (0, 0))
    whole_block = lambda shape: pl.BlockSpec(shape, lambda i: (0, 0))
    scalar_block = pl.BlockSpec(memory_space=pltpu.SMEM)
    new_first, new_second, raw, sums = pl.pallas_call(
        functools.partial(moments_kernel, width, parts),
        grid=(1,),
        out_shape=(row, row, dense, jax.ShapeDtypeStruct((16, 128), jnp.float32)),
        in_specs=[scalar_block, row_block, row_block, row_block, row_block],
        out_specs=(row_block, row_block, whole_block((rows, 128)), whole_block((16, 128))),
    )(tensor_order, weights, moment_first, moment_second, gradients)
    total = tree_sum(tree_sum(sums, "dp"), "mp")
    scaled_update, new_weights, piece = pl.pallas_call(
        functools.partial(update_kernel, width, parts),
        grid=(1,),
        out_shape=(row, row, jax.ShapeDtypeStruct((rows, 128), jnp.bfloat16)),
        in_specs=[scalar_block, whole_block((16, 128)), row_block, whole_block((rows, 128))],
        out_specs=(row_block, row_block, whole_block((rows, 128))),
    )(tensor_order, total, weights, raw)
    whole = lax.all_gather(piece, "dp", axis=0, tiled=False)
    training_copy = assemble(whole, width)
    sums_by_slot = jnp.sum(total, axis=1)
    matches = tensor_order[:, None] == jnp.arange(SLOTS, dtype=jnp.int32)[None, :]
    wsq = jnp.sum(jnp.where(matches, sums_by_slot[:SLOTS, None], 0.0), axis=0)
    usq = jnp.sum(jnp.where(matches, sums_by_slot[8 : 8 + SLOTS, None], 0.0), axis=0)
    trust = jnp.sqrt(wsq) / (jnp.sqrt(usq) + 1e-06)
    return (new_weights, new_first, new_second, scaled_update, training_copy, trust)


def solution(mesh):
    return jax.shard_map(
        on_device,
        mesh=mesh,
        in_specs=(P("mp", "dp"), P("mp", "dp"), P("mp", "dp"), P("mp", "dp"), P()),
        out_specs=(P("mp", "dp"), P("mp", "dp"), P("mp", "dp"), P("mp", "dp"), P("mp", None), P()),
        check_vma=False,
    )
```

```python
import functools
import math

import jax
import jax.numpy as jnp
from jax import lax
from jax.experimental import pallas as pl
from jax.experimental.pallas import tpu as pltpu
from jax.sharding import PartitionSpec as P

D = 2304
EXPERTS = 8
SLOTS = 7


fix_first = 1.0 - math.exp(1000.0 * math.log(0.9))
fix_second = 1.0 - math.exp(1000.0 * math.log(0.999))
decay_values = (0.01, 0.01, 0.01, 0.01, 0.0, 0.0, 0.0)
step_rate = 0.1


def tensor_kind(places, order, parts):
    lengths = jnp.array(
        [D * D // parts] * 4 + [EXPERTS * D // parts, D // parts, D // parts], jnp.int32
    )
    kinds = jnp.arange(SLOTS, dtype=jnp.int32)
    slot_lengths = jnp.sum(jnp.where(order[:, None] == kinds[None, :], lengths[None, :], 0), axis=1)
    boundary = jnp.cumsum(slot_lengths)
    slot = jnp.zeros_like(places)
    for number in range(SLOTS - 1):
        slot = slot + (places >= boundary[number]).astype(jnp.int32)
    result = jnp.zeros_like(places)
    for number in range(SLOTS):
        result = jnp.where(slot == number, order[number], result)
    return result


def per_entry(kind, table):
    result = jnp.zeros(kind.shape, jnp.float32)
    for number in range(SLOTS):
        result = jnp.where(kind == number, table[number], result)
    return result


def kind_sums(kind, values):
    kinds = jnp.arange(SLOTS, dtype=jnp.int32)[:, None, None]
    return jnp.sum(jnp.where(kind[None] == kinds, values[None], 0.0), axis=1)


GRAY = (0, 1, 3, 2)
RING8 = (0, 1, 2, 3, 6, 7, 4, 5)


def partner(index, step, size):
    if size != 32:
        return index ^ step
    core, x, y = index % 2, (index // 2) % 4, index // 8
    if step == 1:
        core ^= 1
    elif step < 8:
        x = GRAY[GRAY[x] ^ (step // 2)]
    else:
        y = GRAY[GRAY[y] ^ (step // 8)]
    return (y * 4 + x) * 2 + core


def tree_sum(x, axis):
    size = lax.axis_size(axis)
    step = 1
    while step < size:
        if axis == "dp":
            pairs = [(i, partner(i, step, size)) for i in range(size)]
        elif size == 8:
            pairs = [(i, RING8.index(RING8[i] ^ step)) for i in range(size)]
        else:
            pairs = [(i, i ^ step) for i in range(size)]
        x = x + lax.ppermute(x, axis, pairs)
        step *= 2
    return x


def to_dense(row, padded):
    return jnp.pad(row, ((0, 0), (0, padded - row.shape[1]))).reshape(padded // 128, 128)


def from_dense(block, width):
    return block.reshape(1, -1)[:, :width]


def slot_of(order_ref, width, parts, rows):
    lengths = [D * D // parts] * 4 + [EXPERTS * D // parts, D // parts, D // parts]
    places = (
        lax.axis_index("dp") * width
        + lax.broadcasted_iota(jnp.int32, (rows, 128), 0) * 128
        + lax.broadcasted_iota(jnp.int32, (rows, 128), 1)
    )
    slot = jnp.zeros((rows, 128), jnp.int32)
    boundary = jnp.int32(0)
    for number in range(SLOTS - 1):
        kind = order_ref[number]
        length = jnp.int32(lengths[SLOTS - 1])
        for other in range(SLOTS - 1):
            length = jnp.where(kind == other, jnp.int32(lengths[other]), length)
        boundary = boundary + length
        slot = slot + (places >= boundary).astype(jnp.int32)
    return slot


def decay_of(order_ref, slot):
    result = jnp.zeros(slot.shape, jnp.float32)
    for number in range(SLOTS):
        kind = order_ref[number]
        value = jnp.float32(0.0)
        for other in range(SLOTS):
            value = jnp.where(kind == other, jnp.float32(decay_values[other]), value)
        result = jnp.where(slot == number, value, result)
    return result


def load_dense(row_ref, rows, width):
    block = row_ref[...].astype(jnp.float32).reshape(rows, 128)
    inside = (
        lax.broadcasted_iota(jnp.int32, (rows, 128), 0) * 128
        + lax.broadcasted_iota(jnp.int32, (rows, 128), 1)
    ) < width
    return jnp.where(inside, block, 0.0)


def store_row(row_ref, block):
    row_ref[...] = block.reshape(row_ref.shape).astype(row_ref.dtype)


def moments_kernel(width, parts, order_ref, w_ref, m1_ref, m2_ref, g_ref, nf_ref, ns_ref, raw_ref, sums_ref):
    rows = raw_ref.shape[0]
    slot = slot_of(order_ref, width, parts, rows)
    grads = load_dense(g_ref, rows, width)
    new_first = 0.9 * load_dense(m1_ref, rows, width) + 0.1 * grads
    new_second = 0.999 * load_dense(m2_ref, rows, width) + 0.001 * grads * grads
    w = load_dense(w_ref, rows, width)
    raw = new_first / fix_first / (jnp.sqrt(new_second / fix_second) + 1e-06) + decay_of(order_ref, slot) * w
    store_row(nf_ref, new_first)
    store_row(ns_ref, new_second)
    raw_ref[...] = raw
    wsq = w * w
    usq = raw * raw
    sums_ref[...] = jnp.zeros(sums_ref.shape, jnp.float32)
    for number in range(SLOTS):
        mask = slot == number
        sums_ref[pl.ds(number, 1), :] = jnp.sum(jnp.where(mask, wsq, 0.0), axis=0, keepdims=True)
        sums_ref[pl.ds(8 + number, 1), :] = jnp.sum(jnp.where(mask, usq, 0.0), axis=0, keepdims=True)


def update_kernel(width, parts, order_ref, total_ref, w_ref, raw_ref, su_ref, nw_ref, tc_ref):
    rows = raw_ref.shape[0]
    slot = slot_of(order_ref, width, parts, rows)
    sums = jnp.sum(total_ref[...], axis=1, keepdims=True)
    trust = jnp.sqrt(sums[:8]) / (jnp.sqrt(sums[8:]) + 1e-06)
    factor = jnp.zeros((rows, 128), jnp.float32)
    for number in range(SLOTS):
        factor = jnp.where(slot == number, trust[number : number + 1, :], factor)
    scaled_update = factor * raw_ref[...]
    new_weights = load_dense(w_ref, rows, width) - step_rate * scaled_update
    store_row(su_ref, scaled_update)
    store_row(nw_ref, new_weights)
    tc_ref[...] = new_weights.astype(jnp.bfloat16)


def assemble_kernel(width, whole_ref, out_ref, stage_ref, sems):
    count, rows, _ = whole_ref.shape
    total = count * width
    lane = lax.broadcasted_iota(jnp.int32, (rows, 128), 1)
    copies = []
    for k in range(count):
        start, shift = divmod(k * width, 128)
        chunks = -(-(shift + width) // 128)
        piece = whole_ref[k].astype(jnp.float32)
        if shift:
            rolled = pltpu.roll(piece, shift, 1)
            piece = jnp.where(lane >= shift, rolled, pltpu.roll(rolled, 1, 0))
        if shift and k:
            held = stage_ref[:, pl.ds(start * 128, 128)].astype(jnp.float32)
            first = jnp.where(lane[:1] >= shift, piece[:1], held)
            piece = jnp.concatenate([first, piece[1:]], axis=0)
        full = min(chunks, total // 128 - start)
        stage_ref[:, pl.ds(start * 128, full * 128)] = piece[:full].reshape(1, full * 128).astype(stage_ref.dtype)
        tail = total - (start + full) * 128
        if full < chunks and tail:
            stage_ref[:, pl.ds((start + full) * 128, tail)] = piece[full : full + 1, :tail].astype(stage_ref.dtype)
        if k + 1 < count:
            end = ((k + 1) * width) // 128 * 128
        else:
            end = total
        begin = 0 if k == 0 else copies_end
        copy = pltpu.make_async_copy(
            stage_ref.at[:, pl.ds(begin, end - begin)], out_ref.at[:, pl.ds(begin, end - begin)], sems.at[k]
        )
        copy.start()
        copies.append(copy)
        copies_end = end
    for copy in copies:
        copy.wait()


def assemble(whole, width):
    count = whole.shape[0]
    return pl.pallas_call(
        functools.partial(assemble_kernel, width),
        out_shape=jax.ShapeDtypeStruct((1, count * width), jnp.bfloat16),
        in_specs=[pl.BlockSpec(memory_space=pltpu.VMEM)],
        out_specs=pl.BlockSpec(memory_space=pl.ANY),
        scratch_shapes=[pltpu.VMEM((1, count * width), jnp.bfloat16), pltpu.SemaphoreType.DMA((count,))],
    )(whole)


def on_device(weights, moment_first, moment_second, gradients, tensor_order):
    parts = lax.axis_size("mp")
    width = weights.shape[1]
    padded = -(-width // 2048) * 2048
    rows = padded // 128
    dense = jax.ShapeDtypeStruct((rows, 128), jnp.float32)
    row = jax.ShapeDtypeStruct((1, width), jnp.float32)
    row_block = pl.BlockSpec((1, padded), lambda i: (0, 0))
    whole_block = lambda shape: pl.BlockSpec(shape, lambda i: (0, 0))
    scalar_block = pl.BlockSpec(memory_space=pltpu.SMEM)
    new_first, new_second, raw, sums = pl.pallas_call(
        functools.partial(moments_kernel, width, parts),
        grid=(1,),
        out_shape=(row, row, dense, jax.ShapeDtypeStruct((16, 128), jnp.float32)),
        in_specs=[scalar_block, row_block, row_block, row_block, row_block],
        out_specs=(row_block, row_block, whole_block((rows, 128)), whole_block((16, 128))),
    )(tensor_order, weights, moment_first, moment_second, gradients)
    total = tree_sum(tree_sum(sums, "dp"), "mp")
    scaled_update, new_weights, piece = pl.pallas_call(
        functools.partial(update_kernel, width, parts),
        grid=(1,),
        out_shape=(row, row, jax.ShapeDtypeStruct((rows, 128), jnp.bfloat16)),
        in_specs=[scalar_block, whole_block((16, 128)), row_block, whole_block((rows, 128))],
        out_specs=(row_block, row_block, whole_block((rows, 128))),
    )(tensor_order, total, weights, raw)
    whole = lax.all_gather(piece, "dp", axis=0, tiled=False)
    training_copy = assemble(whole, width)
    sums_by_slot = jnp.sum(total, axis=1)
    matches = tensor_order[:, None] == jnp.arange(SLOTS, dtype=jnp.int32)[None, :]
    wsq = jnp.sum(jnp.where(matches, sums_by_slot[:SLOTS, None], 0.0), axis=0)
    usq = jnp.sum(jnp.where(matches, sums_by_slot[8 : 8 + SLOTS, None], 0.0), axis=0)
    trust = jnp.sqrt(wsq) / (jnp.sqrt(usq) + 1e-06)
    return (new_weights, new_first, new_second, scaled_update, training_copy, trust)


def solution(mesh):
    return jax.shard_map(
        on_device,
        mesh=mesh,
        in_specs=(P("mp", "dp"), P("mp", "dp"), P("mp", "dp"), P("mp", "dp"), P()),
        out_specs=(P("mp", "dp"), P("mp", "dp"), P("mp", "dp"), P("mp", "dp"), P("mp", None), P()),
        check_vma=False,
    )
```

```python
import functools
import math

import jax
import jax.numpy as jnp
from jax import lax
from jax.experimental import pallas as pl
from jax.experimental.pallas import tpu as pltpu
from jax.sharding import PartitionSpec as P

D = 2304
EXPERTS = 8
SLOTS = 7


fix_first = 1.0 - math.exp(1000.0 * math.log(0.9))
fix_second = 1.0 - math.exp(1000.0 * math.log(0.999))
decay_values = (0.01, 0.01, 0.01, 0.01, 0.0, 0.0, 0.0)
step_rate = 0.1


def tensor_kind(places, order, parts):
    lengths = jnp.array(
        [D * D // parts] * 4 + [EXPERTS * D // parts, D // parts, D // parts], jnp.int32
    )
    kinds = jnp.arange(SLOTS, dtype=jnp.int32)
    slot_lengths = jnp.sum(jnp.where(order[:, None] == kinds[None, :], lengths[None, :], 0), axis=1)
    boundary = jnp.cumsum(slot_lengths)
    slot = jnp.zeros_like(places)
    for number in range(SLOTS - 1):
        slot = slot + (places >= boundary[number]).astype(jnp.int32)
    result = jnp.zeros_like(places)
    for number in range(SLOTS):
        result = jnp.where(slot == number, order[number], result)
    return result


def per_entry(kind, table):
    result = jnp.zeros(kind.shape, jnp.float32)
    for number in range(SLOTS):
        result = jnp.where(kind == number, table[number], result)
    return result


def kind_sums(kind, values):
    kinds = jnp.arange(SLOTS, dtype=jnp.int32)[:, None, None]
    return jnp.sum(jnp.where(kind[None] == kinds, values[None], 0.0), axis=1)


GRAY = (0, 1, 3, 2)
RING8 = (0, 1, 2, 3, 6, 7, 4, 5)


def partner(index, step, size):
    if size != 32:
        return index ^ step
    core, x, y = index % 2, (index // 2) % 4, index // 8
    if step == 1:
        core ^= 1
    elif step < 8:
        x = GRAY[GRAY[x] ^ (step // 2)]
    else:
        y = GRAY[GRAY[y] ^ (step // 8)]
    return (y * 4 + x) * 2 + core


def tree_sum(x, axis, keep_last=False):
    size = lax.axis_size(axis)
    step = 1
    while step < size:
        if axis == "dp":
            pairs = [(i, partner(i, step, size)) for i in range(size)]
        elif size == 8:
            pairs = [(i, RING8.index(RING8[i] ^ step)) for i in range(size)]
        else:
            pairs = [(i, i ^ step) for i in range(size)]
        received = lax.ppermute(x, axis, pairs)
        if keep_last and step * 2 >= size:
            return x, received
        x = x + received
        step *= 2
    return x


def to_dense(row, padded):
    return jnp.pad(row, ((0, 0), (0, padded - row.shape[1]))).reshape(padded // 128, 128)


def from_dense(block, width):
    return block.reshape(1, -1)[:, :width]


def slot_of(order_ref, width, parts, rows):
    lengths = [D * D // parts] * 4 + [EXPERTS * D // parts, D // parts, D // parts]
    places = (
        lax.axis_index("dp") * width
        + lax.broadcasted_iota(jnp.int32, (rows, 128), 0) * 128
        + lax.broadcasted_iota(jnp.int32, (rows, 128), 1)
    )
    slot = jnp.zeros((rows, 128), jnp.int32)
    boundary = jnp.int32(0)
    for number in range(SLOTS - 1):
        kind = order_ref[number]
        length = jnp.int32(lengths[SLOTS - 1])
        for other in range(SLOTS - 1):
            length = jnp.where(kind == other, jnp.int32(lengths[other]), length)
        boundary = boundary + length
        slot = slot + (places >= boundary).astype(jnp.int32)
    return slot


def decay_of(order_ref, slot):
    result = jnp.zeros(slot.shape, jnp.float32)
    for number in range(SLOTS):
        kind = order_ref[number]
        value = jnp.float32(0.0)
        for other in range(SLOTS):
            value = jnp.where(kind == other, jnp.float32(decay_values[other]), value)
        result = jnp.where(slot == number, value, result)
    return result


def load_dense(row_ref, rows, width):
    block = row_ref[...].astype(jnp.float32).reshape(rows, 128)
    inside = (
        lax.broadcasted_iota(jnp.int32, (rows, 128), 0) * 128
        + lax.broadcasted_iota(jnp.int32, (rows, 128), 1)
    ) < width
    return jnp.where(inside, block, 0.0)


def store_row(row_ref, block):
    row_ref[...] = block.reshape(row_ref.shape).astype(row_ref.dtype)


def moments_kernel(width, parts, order_ref, w_ref, m1_ref, m2_ref, g_ref, nf_ref, ns_ref, raw_ref, sums_ref):
    rows = raw_ref.shape[0]
    slot = slot_of(order_ref, width, parts, rows)
    grads = load_dense(g_ref, rows, width)
    new_first = 0.9 * load_dense(m1_ref, rows, width) + 0.1 * grads
    new_second = 0.999 * load_dense(m2_ref, rows, width) + 0.001 * grads * grads
    w = load_dense(w_ref, rows, width)
    raw = new_first / fix_first / (jnp.sqrt(new_second / fix_second) + 1e-06) + decay_of(order_ref, slot) * w
    store_row(nf_ref, new_first)
    store_row(ns_ref, new_second)
    raw_ref[...] = raw
    wsq = w * w
    usq = raw * raw
    sums_ref[...] = jnp.zeros(sums_ref.shape, jnp.float32)
    for number in range(SLOTS):
        mask = slot == number
        sums_ref[pl.ds(number, 1), :] = jnp.sum(jnp.where(mask, wsq, 0.0), axis=0, keepdims=True)
        sums_ref[pl.ds(8 + number, 1), :] = jnp.sum(jnp.where(mask, usq, 0.0), axis=0, keepdims=True)


def update_kernel(width, parts, order_ref, held_ref, received_ref, w_ref, raw_ref, su_ref, nw_ref, tc_ref):
    rows = raw_ref.shape[0]
    slot = slot_of(order_ref, width, parts, rows)
    sums = jnp.sum(held_ref[...] + received_ref[...], axis=1, keepdims=True)
    trust = jnp.sqrt(sums[:8]) / (jnp.sqrt(sums[8:]) + 1e-06)
    factor = jnp.zeros((rows, 128), jnp.float32)
    for number in range(SLOTS):
        factor = jnp.where(slot == number, trust[number : number + 1, :], factor)
    scaled_update = factor * raw_ref[...]
    new_weights = load_dense(w_ref, rows, width) - step_rate * scaled_update
    store_row(su_ref, scaled_update)
    store_row(nw_ref, new_weights)
    tc_ref[...] = new_weights.astype(jnp.bfloat16)


def assemble_kernel(width, whole_ref, out_ref, stage_ref, sems):
    count, rows, _ = whole_ref.shape
    total = count * width
    lane = lax.broadcasted_iota(jnp.int32, (rows, 128), 1)
    copies = []
    for k in range(count):
        start, shift = divmod(k * width, 128)
        chunks = -(-(shift + width) // 128)
        piece = whole_ref[k].astype(jnp.float32)
        if shift:
            rolled = pltpu.roll(piece, shift, 1)
            piece = jnp.where(lane >= shift, rolled, pltpu.roll(rolled, 1, 0))
        if shift and k:
            held = stage_ref[:, pl.ds(start * 128, 128)].astype(jnp.float32)
            first = jnp.where(lane[:1] >= shift, piece[:1], held)
            piece = jnp.concatenate([first, piece[1:]], axis=0)
        full = min(chunks, total // 128 - start)
        stage_ref[:, pl.ds(start * 128, full * 128)] = piece[:full].reshape(1, full * 128).astype(stage_ref.dtype)
        tail = total - (start + full) * 128
        if full < chunks and tail:
            stage_ref[:, pl.ds((start + full) * 128, tail)] = piece[full : full + 1, :tail].astype(stage_ref.dtype)
        if k + 1 < count:
            end = ((k + 1) * width) // 128 * 128
        else:
            end = total
        begin = 0 if k == 0 else copies_end
        copy = pltpu.make_async_copy(
            stage_ref.at[:, pl.ds(begin, end - begin)], out_ref.at[:, pl.ds(begin, end - begin)], sems.at[k]
        )
        copy.start()
        copies.append(copy)
        copies_end = end
    for copy in copies:
        copy.wait()


def assemble(whole, width):
    count = whole.shape[0]
    return pl.pallas_call(
        functools.partial(assemble_kernel, width),
        out_shape=jax.ShapeDtypeStruct((1, count * width), jnp.bfloat16),
        in_specs=[pl.BlockSpec(memory_space=pltpu.VMEM)],
        out_specs=pl.BlockSpec(memory_space=pl.ANY),
        scratch_shapes=[pltpu.VMEM((1, count * width), jnp.bfloat16), pltpu.SemaphoreType.DMA((count,))],
    )(whole)


def on_device(weights, moment_first, moment_second, gradients, tensor_order):
    parts = lax.axis_size("mp")
    width = weights.shape[1]
    padded = -(-width // 2048) * 2048
    rows = padded // 128
    dense = jax.ShapeDtypeStruct((rows, 128), jnp.float32)
    row = jax.ShapeDtypeStruct((1, width), jnp.float32)
    row_block = pl.BlockSpec((1, padded), lambda i: (0, 0))
    whole_block = lambda shape: pl.BlockSpec(shape, lambda i: (0, 0))
    scalar_block = pl.BlockSpec(memory_space=pltpu.SMEM)
    new_first, new_second, raw, sums = pl.pallas_call(
        functools.partial(moments_kernel, width, parts),
        grid=(1,),
        out_shape=(row, row, dense, jax.ShapeDtypeStruct((16, 128), jnp.float32)),
        in_specs=[scalar_block, row_block, row_block, row_block, row_block],
        out_specs=(row_block, row_block, whole_block((rows, 128)), whole_block((16, 128))),
    )(tensor_order, weights, moment_first, moment_second, gradients)
    held, received = tree_sum(tree_sum(sums, "dp"), "mp", keep_last=True)
    scaled_update, new_weights, piece = pl.pallas_call(
        functools.partial(update_kernel, width, parts),
        grid=(1,),
        out_shape=(row, row, jax.ShapeDtypeStruct((rows, 128), jnp.bfloat16)),
        in_specs=[scalar_block, whole_block((16, 128)), whole_block((16, 128)), row_block, whole_block((rows, 128))],
        out_specs=(row_block, row_block, whole_block((rows, 128))),
    )(tensor_order, held, received, weights, raw)
    whole = lax.all_gather(piece, "dp", axis=0, tiled=False)
    training_copy = assemble(whole, width)
    sums_by_slot = jnp.sum(held + received, axis=1)
    matches = tensor_order[:, None] == jnp.arange(SLOTS, dtype=jnp.int32)[None, :]
    wsq = jnp.sum(jnp.where(matches, sums_by_slot[:SLOTS, None], 0.0), axis=0)
    usq = jnp.sum(jnp.where(matches, sums_by_slot[8 : 8 + SLOTS, None], 0.0), axis=0)
    trust = jnp.sqrt(wsq) / (jnp.sqrt(usq) + 1e-06)
    return (new_weights, new_first, new_second, scaled_update, training_copy, trust)


def solution(mesh):
    return jax.shard_map(
        on_device,
        mesh=mesh,
        in_specs=(P("mp", "dp"), P("mp", "dp"), P("mp", "dp"), P("mp", "dp"), P()),
        out_specs=(P("mp", "dp"), P("mp", "dp"), P("mp", "dp"), P("mp", "dp"), P("mp", None), P()),
        check_vma=False,
    )
```
